512 devices in a mesh: row: 16 (over z), col: 32 (over y, x, core).
Axes of the slice: x: 4, y: 4, z: 16, core: 2. Of those that a mesh axis runs over, the one named last changes fastest.
Arguments:
- node_feats: bfloat16 [262144, 512], P(('row', 'col')), may hold values from -8 to 8
- source_feats: bfloat16 [4096, 512], P('col'), may hold values from -6 to 6
- nbr_blocks: int32 [2048, 8], P(('row', 'col')), may hold values from 0 to 31
- nbr_count: int32 [2048], P(('row', 'col')), may hold values from 1 to 8
- adj_tiles: bfloat16 [2048, 8, 128, 128], P(('row', 'col')), may hold values from -0.1875 to 0.1875
- pos_index: int32 [262144], P(('row', 'col')), may hold values from 0 to 511
- noise_block_rows: int32 [16], replicated, may hold values from 0 to 15
- w_self: bfloat16 [512, 512], replicated, may hold values from -0.25 to 0.25
- w_neigh: bfloat16 [512, 512], replicated, may hold values from -0.25 to 0.25
Outputs:
- grad_self: float32 [512, 512], replicated
- neighbour_weight_gradient: float32 [512, 512], replicated
- loss: float32 [], replicated
The draws below stay inside these ranges and needn't reach their ends.
All inputs are finite; a program needn't handle non-finite values.
Results may differ from the reference program's by a relative error of at most 0.002.
Values may be sent and summed in bfloat16 or wider, within the bound.
No kernel may reach another device: no remote copies, remote signals or barrier semaphores. Data moves between devices by JAX's collectives and lax.ppermute only.
A program may use at most 64 MiB of HBM per device.

```python
import math
import jax
import jax.numpy as jnp
import numpy as np
from jax import lax

D = 512
BLOCK = 128
NOISE = 128
K = 8
ROWS = 512
NODES = 262144
DBLK = 2048
SRC_BLOCKS = 32
SOURCE_ROW_TOTAL = 4096
ROW_GROUPS = 16
N_ROW = 16
N_COL = 32


def draw_node_feats(key, part):
    directions = jax.random.normal(jax.random.fold_in(key, 101), (4, D), jnp.float32)
    mixing = jax.random.normal(jax.random.fold_in(key, 1), (NODES, 4), jnp.float32)
    private = jax.random.normal(jax.random.fold_in(key, 2), (NODES, D), jnp.float32)
    shared = mixing[:, 0:1] * directions[0][None, :]
    for component in range(1, 4):
        shared = shared + mixing[:, component:component + 1] * directions[component][None, :]
    feature_matrix = 0.75 * shared + 0.5 * private
    return jnp.clip(feature_matrix, -8.0, 8.0).astype(jnp.bfloat16)


def touch_ends(entries, own_key, smallest, largest):
    dims = entries.shape
    spot = [jax.random.randint(jax.random.fold_in(own_key, axis), (), 0, dims[axis]) for axis in range(len(dims))]
    entries = entries.at[tuple(spot)].set(smallest)
    longest = dims.index(max(dims))
    spot[longest] = (spot[longest] + 1) % dims[longest]
    return entries.at[tuple(spot)].set(largest)


def block_levels(key, extent, split, low, top_value):
    loudness = 1.0
    for position, shards_of in split:
        draws = jax.random.uniform(jax.random.fold_in(jax.random.fold_in(key, 6), position), (shards_of,), jnp.float32, low / len(split), top_value / len(split))
        loudness = loudness * jnp.repeat(jnp.exp(draws), extent[position] // shards_of).reshape((-1,) + (1,) * (len(extent) - 1 - position))
    return loudness


def rank_bounds(amount, lean):
    weights = [(1 << 20) // math.isqrt(grade ** lean) + 1 for grade in range(1, amount + 1)]
    scale = 1 + sum(weights) // (1 << 30)
    return np.cumsum(np.array([max(1, weight // scale) for weight in weights]))


def ranked(key, extent, number_of, skew):
    grid = rank_bounds(number_of, skew)
    pick = jax.random.randint(jax.random.fold_in(key, 1), extent, 0, int(grid[number_of - 1]))
    standing = jnp.searchsorted(jnp.asarray(grid, jnp.int32), pick, side="right")
    return jax.random.permutation(jax.random.fold_in(key, 2), number_of)[standing].astype(jnp.int32)


def gaussian(rng, extent, scale, reach, cuts=(), held_as=jnp.bfloat16):
    loudness = block_levels(rng, extent, cuts, -0.22, 0.18) if cuts else 1.0
    result = jax.random.normal(rng, extent, jnp.float32) * scale * loudness
    return jnp.minimum(jnp.maximum(result, -reach), reach).astype(held_as)


def setup_inputs(seed: int = 0) -> dict:
    streams_of = jax.random.split(jax.random.key(seed), 10)
    node_feats = draw_node_feats(jax.random.fold_in(streams_of[9], 71), 0)
    source_feats = gaussian(streams_of[1], (SOURCE_ROW_TOTAL, D), 1.0, 6.0, ((0, 32),))
    nbr_blocks = touch_ends(ranked(streams_of[2], (DBLK, K), SRC_BLOCKS, 2), jax.random.fold_in(streams_of[2], 3), 0, SRC_BLOCKS - 1).astype(jnp.int32)
    nbr_count = touch_ends(jax.random.randint(streams_of[3], (DBLK,), 1, K + 1), jax.random.fold_in(streams_of[3], 1), 1, K).astype(jnp.int32)
    adj_tiles = gaussian(streams_of[4], (DBLK, K, BLOCK, BLOCK), (K * BLOCK) ** -0.5, 0.1875, ((0, 512),))
    pos_index = touch_ends(jax.random.randint(streams_of[5], (NODES,), 0, ROWS), jax.random.fold_in(streams_of[5], 1), 0, ROWS - 1).astype(jnp.int32)
    noise_block_rows = touch_ends(jax.random.randint(streams_of[6], (ROW_GROUPS,), 0, ROW_GROUPS), jax.random.fold_in(streams_of[6], 1), 0, ROW_GROUPS - 1).astype(jnp.int32)
    w_self = gaussian(streams_of[7], (D, D), D ** -0.5, 0.25)
    w_neigh = gaussian(streams_of[8], (D, D), D ** -0.5, 0.25)
    return {"node_feats": node_feats, "source_feats": source_feats, "nbr_blocks": nbr_blocks, "nbr_count": nbr_count, "adj_tiles": adj_tiles, "pos_index": pos_index, "noise_block_rows": noise_block_rows, "w_self": w_self, "w_neigh": w_neigh}


softness_divisor = 0.2

def embed(pre):
    return pre * lax.rsqrt(lax.optimization_barrier(jnp.sum(pre * pre, axis=-1, keepdims=True)) + 1e-06)

def reference(node_feats, source_feats, nbr_blocks, nbr_count, adj_tiles, pos_index, noise_block_rows, w_self, w_neigh):
    width = node_feats.shape[1]
    devices = N_ROW * N_COL
    blocks_dev = ROWS // BLOCK
    highest = lax.Precision.HIGHEST
    sources = source_feats.reshape(SRC_BLOCKS, BLOCK, width).astype(jnp.float32)
    slot_ids = jnp.arange(K, dtype=jnp.int32)

    def aggregate(inputs):
        tiles, chosen, counts = inputs
        valid = (slot_ids[None, :] < counts[:, None]).astype(jnp.float32)
        picked = sources[chosen]
        weighted = tiles.astype(jnp.float32) * valid[:, :, None, None]
        return jnp.einsum('bkij,bkjd->bid', weighted, picked, precision=highest)
    agg = lax.map(aggregate, (adj_tiles.reshape(devices, blocks_dev, K, BLOCK, BLOCK), nbr_blocks.reshape(devices, blocks_dev, K), nbr_count.reshape(devices, blocks_dev)))
    agg = agg.reshape(NODES, width).astype(jnp.bfloat16)
    pre = jnp.dot(node_feats, w_self, preferred_element_type=jnp.float32) + jnp.dot(agg, w_neigh, preferred_element_type=jnp.float32)
    emb32, pull = jax.vjp(embed, pre)
    zeta = emb32.astype(jnp.bfloat16).astype(jnp.float32).reshape(N_ROW, N_COL, ROWS, width)
    scale_factor = 1.0 / softness_divisor
    partner_idx = pos_index.reshape(N_ROW, N_COL, ROWS)
    partner = jnp.take_along_axis(zeta, partner_idx[..., None], axis=2)
    s_pos = lax.optimization_barrier(jnp.sum(zeta * partner, axis=-1)) * scale_factor
    noise_emb = zeta[noise_block_rows, :, :NOISE]
    s_neg = jnp.einsum('rcud,rcmd->rcum', zeta, noise_emb, precision=highest) * scale_factor
    loss = (jnp.sum(jax.nn.softplus(-s_pos)) + jnp.sum(jax.nn.softplus(s_neg)) / NOISE) / NODES
    grad_pos = -jax.nn.sigmoid(-s_pos) / NODES
    grad_neg = jax.nn.sigmoid(s_neg) / (NOISE * NODES)
    anchor = scale_factor * (grad_pos[..., None] * partner + jnp.einsum('rcum,rcmd->rcud', grad_neg, noise_emb, precision=highest))
    contrib = (scale_factor * grad_pos[..., None] * zeta).reshape(NODES, width)
    global_idx = (jnp.arange(devices, dtype=jnp.int32)[:, None] * ROWS + partner_idx.reshape(devices, ROWS)).reshape(NODES)
    partner_grad = jax.ops.segment_sum(contrib, global_idx, num_segments=NODES).reshape(N_ROW, N_COL, ROWS, width)
    dnoise = (scale_factor * jnp.einsum('rcum,rcud->rcmd', grad_neg, zeta, precision=highest)).astype(jnp.bfloat16)
    dnoise = lax.optimization_barrier(dnoise).astype(jnp.float32)
    owner = (noise_block_rows[:, None] == jnp.arange(N_ROW, dtype=jnp.int32)[None, :]).astype(jnp.float32)
    returned = jnp.einsum('rs,rcmd->scmd', owner, dnoise, precision=highest)
    dzeta = anchor + partner_grad
    dzeta = dzeta.at[:, :, :NOISE].add(returned)
    gpre = pull(dzeta.reshape(NODES, width))[0].astype(jnp.bfloat16)
    grad_self = jnp.dot(node_feats.T, gpre, preferred_element_type=jnp.float32)
    neighbour_weight_gradient = jnp.dot(agg.T, gpre, preferred_element_type=jnp.float32)
    return (grad_self, neighbour_weight_gradient, loss)
```

```python
import jax
import jax.numpy as jnp
from jax import lax
from jax.sharding import PartitionSpec as P

BLOCK = 128
NOISE = 128


softness_divisor = 0.2


def xor_pairs(size, mask):
    return [(i, i ^ mask) for i in range(size)]


REDUCE_STEPS = (("col", 1), ("col", 2), ("col", 4), ("col", 8), ("col", 16), ("row", 1), ("row", 2), ("row", 4), ("row", 8))


def tree_allreduce(buf, extra):
    taken = []
    for axis, mask in REDUCE_STEPS:
        size = lax.axis_size(axis)
        if mask >= size:
            continue
        bit = (lax.axis_index(axis) // mask) % 2
        half = buf.shape[0] // 2
        keep = lax.dynamic_slice_in_dim(buf, bit * half, half, 0)
        send = lax.dynamic_slice_in_dim(buf, (1 - bit) * half, half, 0)
        got, got_extra = lax.ppermute((send, extra), axis, xor_pairs(size, mask))
        buf = keep + got
        extra = extra + got_extra
        taken.append((axis, mask, bit))
    for axis, mask, bit in reversed(taken):
        size = lax.axis_size(axis)
        got = lax.ppermute(buf, axis, xor_pairs(size, mask))
        rows = buf.shape[0]
        out = jnp.zeros((2 * rows,) + buf.shape[1:], buf.dtype)
        out = lax.dynamic_update_slice_in_dim(out, buf, bit * rows, 0)
        out = lax.dynamic_update_slice_in_dim(out, got, (1 - bit) * rows, 0)
        buf = out
    return buf, extra


def embed(pre):
    return pre * lax.rsqrt(jnp.sum(pre * pre, axis=-1, keepdims=True) + 1e-06)


def body(
    node_feats,
    source_feats,
    nbr_blocks,
    nbr_count,
    adj_tiles,
    pos_index,
    noise_block_rows,
    w_self,
    w_neigh,
):
    rows = node_feats.shape[0]
    width = node_feats.shape[1]
    slots = adj_tiles.shape[1]
    highest = lax.Precision.HIGHEST
    nodes = rows * lax.axis_size("row") * lax.axis_size("col")
    scale_factor = 1.0 / softness_divisor
    valid = jnp.arange(slots, dtype=jnp.int32)[None, :] < nbr_count[:, None]
    tiles = adj_tiles * valid[:, :, None, None].astype(jnp.bfloat16)
    piece = lax.all_gather(source_feats, "col", axis=0, tiled=True)
    count = piece.shape[0] // BLOCK
    blocks = piece.reshape(count, BLOCK, width)
    indicator_matrix = (
        nbr_blocks[:, :, None] == jnp.arange(count, dtype=jnp.int32)[None, None, :]
    ).astype(jnp.bfloat16)
    selected = jnp.einsum(
        "bkc,cjd->bkjd", indicator_matrix, blocks, preferred_element_type=jnp.float32
    ).astype(jnp.bfloat16)
    summed = jnp.einsum("bkij,bkjd->bid", tiles, selected, preferred_element_type=jnp.float32)
    agg = summed.reshape(rows, width).astype(jnp.bfloat16)
    pre = jnp.dot(node_feats, w_self, preferred_element_type=jnp.float32) + jnp.dot(
        agg, w_neigh, preferred_element_type=jnp.float32
    )
    emb32, pull = jax.vjp(embed, pre)
    zeta_bf = emb32.astype(jnp.bfloat16)
    candidates = lax.all_gather(zeta_bf[:NOISE], "row", axis=0, tiled=True)
    my_row = lax.axis_index("row")
    my_noise = noise_block_rows[my_row]
    noise_emb = lax.dynamic_slice_in_dim(candidates, my_noise * NOISE, NOISE, 0).astype(jnp.float32)
    zeta = zeta_bf.astype(jnp.float32)
    pairing = (pos_index[:, None] == jnp.arange(rows, dtype=jnp.int32)[None, :]).astype(jnp.float32)
    partner = jnp.dot(pairing, zeta, precision=highest)
    s_pos = jnp.sum(zeta * partner, axis=-1) * scale_factor
    s_neg = jnp.dot(zeta, noise_emb.T, precision=highest) * scale_factor
    loss_part = (jnp.sum(jax.nn.softplus(-s_pos)) + jnp.sum(jax.nn.softplus(s_neg)) / NOISE) / nodes
    grad_pos = -jax.nn.sigmoid(-s_pos) / nodes
    grad_neg = jax.nn.sigmoid(s_neg) / (NOISE * nodes)
    anchor = scale_factor * (
        grad_pos[:, None] * partner + jnp.dot(grad_neg, noise_emb, precision=highest)
    )
    partner_grad = jnp.dot(pairing.T, scale_factor * grad_pos[:, None] * zeta, precision=highest)
    dnoise = scale_factor * jnp.dot(grad_neg.T, zeta, precision=highest)
    groups = lax.axis_size("row")
    collected = lax.all_gather(dnoise.astype(jnp.bfloat16), "row", axis=0, tiled=True)
    owned = (noise_block_rows == my_row).astype(jnp.float32)
    returned = jnp.dot(
        owned[None, :],
        collected.astype(jnp.float32).reshape(groups, NOISE * width),
        precision=highest,
    )
    returned = returned.reshape(NOISE, width)
    dzeta = anchor + partner_grad
    dzeta = dzeta.at[:NOISE].add(returned)
    gpre = pull(dzeta)[0].astype(jnp.bfloat16)
    part_self = jnp.dot(node_feats.T, gpre, preferred_element_type=jnp.float32)
    neighbour_partial = jnp.dot(agg.T, gpre, preferred_element_type=jnp.float32)
    stacked = jnp.concatenate([part_self, neighbour_partial], axis=0)
    total, loss_tile = tree_allreduce(stacked, jnp.broadcast_to(loss_part, (8, 128)))
    grad_self = total[:width]
    neighbour_weight_gradient = total[width:]
    return (grad_self, neighbour_weight_gradient, loss_tile[0, 0])


def solution(mesh):
    in_specs = (
        P(("row", "col"), None),
        P("col", None),
        P(("row", "col"), None),
        P(("row", "col")),
        P(("row", "col"), None, None, None),
        P(("row", "col")),
        P(),
        P(),
        P(),
    )
    out_specs = (P(), P(), P())
    return jax.shard_map(body, mesh=mesh, in_specs=in_specs, out_specs=out_specs, check_vma=False)
```

```python
import jax
import jax.numpy as jnp
from jax import lax
from jax.sharding import PartitionSpec as P

BLOCK = 128
NOISE = 128


softness_divisor = 0.2


def xor_pairs(size, mask):
    return [(i, i ^ mask) for i in range(size)]


HALVING = (("col", 1), ("col", 2), ("col", 4), ("col", 8), ("col", 16))
BUTTERFLY = (("row", 1), ("row", 2), ("row", 4), ("row", 8))


def tree_allreduce(buf, extra):
    taken = []
    for axis, mask in HALVING:
        size = lax.axis_size(axis)
        if mask >= size:
            continue
        bit = (lax.axis_index(axis) // mask) % 2
        half = buf.shape[0] // 2
        keep = lax.dynamic_slice_in_dim(buf, bit * half, half, 0)
        send = lax.dynamic_slice_in_dim(buf, (1 - bit) * half, half, 0)
        got = lax.ppermute(jnp.concatenate([send, extra], 0), axis, xor_pairs(size, mask))
        buf = keep + got[:half]
        extra = extra + got[half:]
        taken.append((axis, mask, bit))
    joined = jnp.concatenate([buf, extra], 0)
    for axis, mask in BUTTERFLY:
        size = lax.axis_size(axis)
        if mask >= size:
            continue
        joined = joined + lax.ppermute(joined, axis, xor_pairs(size, mask))
    rows = buf.shape[0]
    buf, extra = joined[:rows], joined[rows:]
    for axis, mask, bit in reversed(taken):
        size = lax.axis_size(axis)
        got = lax.ppermute(buf, axis, xor_pairs(size, mask))
        rows = buf.shape[0]
        out = jnp.zeros((2 * rows,) + buf.shape[1:], buf.dtype)
        out = lax.dynamic_update_slice_in_dim(out, buf, bit * rows, 0)
        out = lax.dynamic_update_slice_in_dim(out, got, (1 - bit) * rows, 0)
        buf = out
    return buf, extra


def embed(pre):
    return pre * lax.rsqrt(jnp.sum(pre * pre, axis=-1, keepdims=True) + 1e-06)


def body(
    node_feats,
    source_feats,
    nbr_blocks,
    nbr_count,
    adj_tiles,
    pos_index,
    noise_block_rows,
    w_self,
    w_neigh,
):
    rows = node_feats.shape[0]
    width = node_feats.shape[1]
    slots = adj_tiles.shape[1]
    highest = lax.Precision.HIGHEST
    nodes = rows * lax.axis_size("row") * lax.axis_size("col")
    scale_factor = 1.0 / softness_divisor
    valid = jnp.arange(slots, dtype=jnp.int32)[None, :] < nbr_count[:, None]
    tiles = adj_tiles * valid[:, :, None, None].astype(jnp.bfloat16)
    piece = lax.all_gather(source_feats, "col", axis=0, tiled=True)
    count = piece.shape[0] // BLOCK
    blocks = piece.reshape(count, BLOCK, width)
    indicator_matrix = (
        nbr_blocks[:, :, None] == jnp.arange(count, dtype=jnp.int32)[None, None, :]
    ).astype(jnp.bfloat16)
    selected = jnp.einsum(
        "bkc,cjd->bkjd", indicator_matrix, blocks, preferred_element_type=jnp.float32
    ).astype(jnp.bfloat16)
    summed = jnp.einsum("bkij,bkjd->bid", tiles, selected, preferred_element_type=jnp.float32)
    agg = summed.reshape(rows, width).astype(jnp.bfloat16)
    pre = jnp.dot(node_feats, w_self, preferred_element_type=jnp.float32) + jnp.dot(
        agg, w_neigh, preferred_element_type=jnp.float32
    )
    emb32, pull = jax.vjp(embed, pre)
    zeta_bf = emb32.astype(jnp.bfloat16)
    candidates = lax.all_gather(zeta_bf[:NOISE], "row", axis=0, tiled=True)
    my_row = lax.axis_index("row")
    my_noise = noise_block_rows[my_row]
    noise_emb = lax.dynamic_slice_in_dim(candidates, my_noise * NOISE, NOISE, 0).astype(jnp.float32)
    zeta = zeta_bf.astype(jnp.float32)
    pairing = (pos_index[:, None] == jnp.arange(rows, dtype=jnp.int32)[None, :]).astype(jnp.float32)
    partner = jnp.dot(pairing, zeta, precision=highest)
    s_pos = jnp.sum(zeta * partner, axis=-1) * scale_factor
    s_neg = jnp.dot(zeta, noise_emb.T, precision=highest) * scale_factor
    loss_part = (jnp.sum(jax.nn.softplus(-s_pos)) + jnp.sum(jax.nn.softplus(s_neg)) / NOISE) / nodes
    grad_pos = -jax.nn.sigmoid(-s_pos) / nodes
    grad_neg = jax.nn.sigmoid(s_neg) / (NOISE * nodes)
    anchor = scale_factor * (
        grad_pos[:, None] * partner + jnp.dot(grad_neg, noise_emb, precision=highest)
    )
    partner_grad = jnp.dot(pairing.T, scale_factor * grad_pos[:, None] * zeta, precision=highest)
    dnoise = scale_factor * jnp.dot(grad_neg.T, zeta, precision=highest)
    groups = lax.axis_size("row")
    collected = lax.all_gather(dnoise.astype(jnp.bfloat16), "row", axis=0, tiled=True)
    owned = (noise_block_rows == my_row).astype(jnp.float32)
    returned = jnp.dot(
        owned[None, :],
        collected.astype(jnp.float32).reshape(groups, NOISE * width),
        precision=highest,
    )
    returned = returned.reshape(NOISE, width)
    dzeta = anchor + partner_grad
    dzeta = dzeta.at[:NOISE].add(returned)
    gpre = pull(dzeta)[0].astype(jnp.bfloat16)
    part_self = jnp.dot(node_feats.T, gpre, preferred_element_type=jnp.float32)
    neighbour_partial = jnp.dot(agg.T, gpre, preferred_element_type=jnp.float32)
    stacked = jnp.concatenate([part_self, neighbour_partial], axis=0)
    total, loss_tile = tree_allreduce(stacked, jnp.broadcast_to(loss_part, (8, width)))
    grad_self = total[:width]
    neighbour_weight_gradient = total[width:]
    return (grad_self, neighbour_weight_gradient, loss_tile[0, 0])


def solution(mesh):
    in_specs = (
        P(("row", "col"), None),
        P("col", None),
        P(("row", "col"), None),
        P(("row", "col")),
        P(("row", "col"), None, None, None),
        P(("row", "col")),
        P(),
        P(),
        P(),
    )
    out_specs = (P(), P(), P())
    return jax.shard_map(body, mesh=mesh, in_specs=in_specs, out_specs=out_specs, check_vma=False)
```

```python
import jax
import jax.numpy as jnp
from jax import lax
from jax.sharding import PartitionSpec as P

BLOCK = 128
NOISE = 128


softness_divisor = 0.2


def xor_pairs(size, mask):
    return [(i, i ^ mask) for i in range(size)]


HALVING = (("col", 1), ("col", 2), ("col", 4), ("col", 8), ("col", 16))
BUTTERFLY = (("row", 1), ("row", 2), ("row", 4), ("row", 8))


def tree_allreduce(buf, extra):
    taken = []
    for axis, mask in HALVING:
        size = lax.axis_size(axis)
        if mask >= size:
            continue
        bit = (lax.axis_index(axis) // mask) % 2
        half = buf.shape[0] // 2
        keep = lax.dynamic_slice_in_dim(buf, bit * half, half, 0)
        send = lax.dynamic_slice_in_dim(buf, (1 - bit) * half, half, 0)
        got = lax.ppermute(jnp.concatenate([send, extra], 0), axis, xor_pairs(size, mask))
        buf = keep + got[:half]
        extra = extra + got[half:]
        taken.append((axis, mask, bit))
    joined = jnp.concatenate([buf, extra], 0)
    for axis, mask in BUTTERFLY:
        size = lax.axis_size(axis)
        if mask >= size:
            continue
        joined = joined + lax.ppermute(joined, axis, xor_pairs(size, mask))
    rows = buf.shape[0]
    buf, extra = joined[:rows], joined[rows:]
    for axis, mask, bit in reversed(taken):
        size = lax.axis_size(axis)
        got = lax.ppermute(buf, axis, xor_pairs(size, mask))
        rows = buf.shape[0]
        out = jnp.zeros((2 * rows,) + buf.shape[1:], buf.dtype)
        out = lax.dynamic_update_slice_in_dim(out, buf, bit * rows, 0)
        out = lax.dynamic_update_slice_in_dim(out, got, (1 - bit) * rows, 0)
        buf = out
    return buf, extra


def embed(pre):
    return pre * lax.rsqrt(jnp.sum(pre * pre, axis=-1, keepdims=True) + 1e-06)


def body(
    node_feats,
    source_feats,
    nbr_blocks,
    nbr_count,
    adj_tiles,
    pos_index,
    noise_block_rows,
    w_self,
    w_neigh,
):
    rows = node_feats.shape[0]
    width = node_feats.shape[1]
    slots = adj_tiles.shape[1]
    lanes = adj_tiles.shape[3]
    highest = lax.Precision.HIGHEST
    groups = lax.axis_size("row")
    nodes = rows * groups * lax.axis_size("col")
    scale_factor = 1.0 / softness_divisor
    valid = jnp.arange(slots, dtype=jnp.int32)[None, :] < nbr_count[:, None]
    tiles = adj_tiles * valid[:, :, None, None].astype(jnp.bfloat16)
    id_row = jnp.zeros((8, lanes), jnp.bfloat16).at[0, :slots].set(nbr_blocks[0].astype(jnp.bfloat16))
    nf_rows = NOISE * width // lanes
    payload = jnp.concatenate(
        [node_feats[:NOISE].reshape(nf_rows, lanes), tiles[0].reshape(slots * BLOCK, lanes), id_row], axis=0
    )
    fanned = jnp.broadcast_to(payload[None], (groups,) + payload.shape)
    arrived = lax.all_to_all(fanned, "row", 0, 0, tiled=False)
    my_row = lax.axis_index("row")
    fetched = lax.dynamic_index_in_dim(arrived, noise_block_rows[my_row], 0, keepdims=False)
    noise_feats = fetched[:nf_rows].reshape(NOISE, width)
    noise_tiles = fetched[nf_rows:nf_rows + slots * BLOCK].reshape(1, slots, BLOCK, BLOCK)
    noise_ids = fetched[nf_rows + slots * BLOCK, :slots].astype(jnp.int32)
    all_tiles = jnp.concatenate([tiles, noise_tiles], axis=0)
    all_ids = jnp.concatenate([nbr_blocks, noise_ids[None]], axis=0)
    all_feats = jnp.concatenate([node_feats, noise_feats], axis=0)
    piece = lax.all_gather(source_feats, "col", axis=0, tiled=True)
    count = piece.shape[0] // BLOCK
    blocks = piece.reshape(count, BLOCK, width)
    indicator_matrix = (
        all_ids[:, :, None] == jnp.arange(count, dtype=jnp.int32)[None, None, :]
    ).astype(jnp.bfloat16)
    selected = jnp.einsum(
        "bkc,cjd->bkjd", indicator_matrix, blocks, preferred_element_type=jnp.float32
    ).astype(jnp.bfloat16)
    summed = jnp.einsum("bkij,bkjd->bid", all_tiles, selected, preferred_element_type=jnp.float32)
    agg = summed.reshape(rows + NOISE, width).astype(jnp.bfloat16)
    pre = jnp.dot(all_feats, w_self, preferred_element_type=jnp.float32) + jnp.dot(
        agg, w_neigh, preferred_element_type=jnp.float32
    )
    emb32, pull = jax.vjp(embed, pre)
    zeta_bf = emb32.astype(jnp.bfloat16)
    noise_emb = zeta_bf[rows:].astype(jnp.float32)
    zeta = zeta_bf[:rows].astype(jnp.float32)
    pairing = (pos_index[:, None] == jnp.arange(rows, dtype=jnp.int32)[None, :]).astype(jnp.float32)
    partner = jnp.dot(pairing, zeta, precision=highest)
    s_pos = jnp.sum(zeta * partner, axis=-1) * scale_factor
    s_neg = jnp.dot(zeta, noise_emb.T, precision=highest) * scale_factor
    loss_part = (jnp.sum(jax.nn.softplus(-s_pos)) + jnp.sum(jax.nn.softplus(s_neg)) / NOISE) / nodes
    grad_pos = -jax.nn.sigmoid(-s_pos) / nodes
    grad_neg = jax.nn.sigmoid(s_neg) / (NOISE * nodes)
    anchor = scale_factor * (
        grad_pos[:, None] * partner + jnp.dot(grad_neg, noise_emb, precision=highest)
    )
    partner_grad = jnp.dot(pairing.T, scale_factor * grad_pos[:, None] * zeta, precision=highest)
    dnoise = scale_factor * jnp.dot(grad_neg.T, zeta, precision=highest)
    dnoise = dnoise.astype(jnp.bfloat16).astype(jnp.float32)
    dzeta = jnp.concatenate([anchor + partner_grad, dnoise], axis=0)
    gpre = pull(dzeta)[0].astype(jnp.bfloat16)
    part_self = jnp.dot(all_feats.T, gpre, preferred_element_type=jnp.float32)
    neighbour_partial = jnp.dot(agg.T, gpre, preferred_element_type=jnp.float32)
    stacked = jnp.concatenate([part_self, neighbour_partial], axis=0)
    total, loss_tile = tree_allreduce(stacked, jnp.broadcast_to(loss_part, (8, width)))
    grad_self = total[:width]
    neighbour_weight_gradient = total[width:]
    return (grad_self, neighbour_weight_gradient, loss_tile[0, 0])


def solution(mesh):
    in_specs = (
        P(("row", "col"), None),
        P("col", None),
        P(("row", "col"), None),
        P(("row", "col")),
        P(("row", "col"), None, None, None),
        P(("row", "col")),
        P(),
        P(),
        P(),
    )
    out_specs = (P(), P(), P())
    return jax.shard_map(body, mesh=mesh, in_specs=in_specs, out_specs=out_specs, check_vma=False)
```

```python
import jax
import jax.numpy as jnp
from jax import lax
from jax.sharding import PartitionSpec as P

BLOCK = 128
NOISE = 128


softness_divisor = 0.2


def xor_pairs(size, mask):
    return [(i, i ^ mask) for i in range(size)]


DOUBLING = (("col", 16), ("col", 8), ("col", 4), ("col", 2), ("col", 1))
BUTTERFLY = (("row", 1), ("row", 2), ("row", 4), ("row", 8))


def tree_allreduce(buf, extra):
    ways = lax.axis_size("col")
    me = lax.axis_index("col")
    masks = [mask for axis, mask in DOUBLING if mask < ways]
    position = [sum(((j // mask) % 2) << t for t, mask in enumerate(masks)) for j in range(ways)]
    rows = buf.shape[0] // ways
    chunks = buf.reshape(ways, rows, buf.shape[1])[jnp.array(position, jnp.int32)]
    chunks = jnp.concatenate([chunks, jnp.broadcast_to(extra[None], (ways,) + extra.shape)], axis=1)
    joined = lax.all_to_all(chunks, "col", 0, 0, tiled=False).sum(axis=0)
    for axis, mask in BUTTERFLY:
        size = lax.axis_size(axis)
        if mask >= size:
            continue
        joined = joined + lax.ppermute(joined, axis, xor_pairs(size, mask))
    buf, extra = joined[:rows], joined[rows:]
    for mask in masks:
        bit = (me // mask) % 2
        got = lax.ppermute(buf, "col", xor_pairs(ways, mask))
        held = buf.shape[0]
        out = jnp.zeros((2 * held,) + buf.shape[1:], buf.dtype)
        out = lax.dynamic_update_slice_in_dim(out, buf, bit * held, 0)
        out = lax.dynamic_update_slice_in_dim(out, got, (1 - bit) * held, 0)
        buf = out
    return buf, extra


def embed(pre):
    return pre * lax.rsqrt(jnp.sum(pre * pre, axis=-1, keepdims=True) + 1e-06)


def body(
    node_feats,
    source_feats,
    nbr_blocks,
    nbr_count,
    adj_tiles,
    pos_index,
    noise_block_rows,
    w_self,
    w_neigh,
):
    rows = node_feats.shape[0]
    width = node_feats.shape[1]
    slots = adj_tiles.shape[1]
    highest = lax.Precision.HIGHEST
    nodes = rows * lax.axis_size("row") * lax.axis_size("col")
    scale_factor = 1.0 / softness_divisor
    valid = jnp.arange(slots, dtype=jnp.int32)[None, :] < nbr_count[:, None]
    tiles = adj_tiles * valid[:, :, None, None].astype(jnp.bfloat16)
    piece = lax.all_gather(source_feats, "col", axis=0, tiled=True)
    count = piece.shape[0] // BLOCK
    blocks = piece.reshape(count, BLOCK, width)
    indicator_matrix = (
        nbr_blocks[:, :, None] == jnp.arange(count, dtype=jnp.int32)[None, None, :]
    ).astype(jnp.bfloat16)
    selected = jnp.einsum(
        "bkc,cjd->bkjd", indicator_matrix, blocks, preferred_element_type=jnp.float32
    ).astype(jnp.bfloat16)
    summed = jnp.einsum("bkij,bkjd->bid", tiles, selected, preferred_element_type=jnp.float32)
    agg = summed.reshape(rows, width).astype(jnp.bfloat16)
    pre = jnp.dot(node_feats, w_self, preferred_element_type=jnp.float32) + jnp.dot(
        agg, w_neigh, preferred_element_type=jnp.float32
    )
    emb32, pull = jax.vjp(embed, pre)
    zeta_bf = emb32.astype(jnp.bfloat16)
    candidates = lax.all_gather(zeta_bf[:NOISE], "row", axis=0, tiled=True)
    my_row = lax.axis_index("row")
    my_noise = noise_block_rows[my_row]
    noise_emb = lax.dynamic_slice_in_dim(candidates, my_noise * NOISE, NOISE, 0).astype(jnp.float32)
    zeta = zeta_bf.astype(jnp.float32)
    pairing = (pos_index[:, None] == jnp.arange(rows, dtype=jnp.int32)[None, :]).astype(jnp.float32)
    partner = jnp.dot(pairing.astype(jnp.bfloat16), zeta_bf, preferred_element_type=jnp.float32)
    s_pos = jnp.sum(zeta * partner, axis=-1) * scale_factor
    s_neg = jnp.dot(zeta_bf, noise_emb.astype(jnp.bfloat16).T, preferred_element_type=jnp.float32) * scale_factor
    loss_part = (jnp.sum(jax.nn.softplus(-s_pos)) + jnp.sum(jax.nn.softplus(s_neg)) / NOISE) / nodes
    grad_pos = -jax.nn.sigmoid(-s_pos) / nodes
    grad_neg = jax.nn.sigmoid(s_neg) / (NOISE * nodes)
    anchor = scale_factor * (
        grad_pos[:, None] * partner + jnp.dot(grad_neg, noise_emb, precision=highest)
    )
    partner_grad = jnp.dot(pairing.T, scale_factor * grad_pos[:, None] * zeta, precision=highest)
    dnoise = scale_factor * jnp.dot(grad_neg.T, zeta, precision=highest)
    groups = lax.axis_size("row")
    collected = lax.all_gather(dnoise.astype(jnp.bfloat16), "row", axis=0, tiled=True)
    owned = (noise_block_rows == my_row).astype(jnp.float32)
    returned = jnp.sum(
        owned[:, None, None] * collected.astype(jnp.float32).reshape(groups, NOISE, width), axis=0
    )
    dzeta = anchor + partner_grad
    dzeta = dzeta.at[:NOISE].add(returned)
    gpre = pull(dzeta)[0].astype(jnp.bfloat16)
    part_self = jnp.dot(node_feats.T, gpre, preferred_element_type=jnp.float32)
    neighbour_partial = jnp.dot(agg.T, gpre, preferred_element_type=jnp.float32)
    stacked = jnp.concatenate([part_self, neighbour_partial], axis=0)
    total, loss_tile = tree_allreduce(stacked, jnp.broadcast_to(loss_part, (8, width)))
    grad_self = total[:width]
    neighbour_weight_gradient = total[width:]
    return (grad_self, neighbour_weight_gradient, loss_tile[0, 0])


def solution(mesh):
    in_specs = (
        P(("row", "col"), None),
        P("col", None),
        P(("row", "col"), None),
        P(("row", "col")),
        P(("row", "col"), None, None, None),
        P(("row", "col")),
        P(),
        P(),
        P(),
    )
    out_specs = (P(), P(), P())
    return jax.shard_map(body, mesh=mesh, in_specs=in_specs, out_specs=out_specs, check_vma=False)
```

```python
import jax
import jax.numpy as jnp
from jax import lax
from jax.sharding import PartitionSpec as P

BLOCK = 128
NOISE = 128


softness_divisor = 0.2


def xor_pairs(size, mask):
    return [(i, i ^ mask) for i in range(size)]


DOUBLING = (("col", 16), ("col", 8), ("col", 4), ("col", 2), ("col", 1))
BUTTERFLY = (("row", 1), ("row", 2), ("row", 4), ("row", 8))


def tree_allreduce(buf, extra):
    ways = lax.axis_size("col")
    me = lax.axis_index("col")
    masks = [mask for axis, mask in DOUBLING if mask < ways]
    position = [sum(((j // mask) % 2) << t for t, mask in enumerate(masks)) for j in range(ways)]
    rows = buf.shape[0] // ways
    chunks = buf.reshape(ways, rows, buf.shape[1])[jnp.array(position, jnp.int32)]
    chunks = jnp.concatenate([chunks, jnp.broadcast_to(extra[None], (ways,) + extra.shape)], axis=1)
    joined = lax.all_to_all(chunks, "col", 0, 0, tiled=False).sum(axis=0)
    for axis, mask in BUTTERFLY:
        size = lax.axis_size(axis)
        if mask >= size:
            continue
        joined = joined + lax.ppermute(joined, axis, xor_pairs(size, mask))
    buf, extra = joined[:rows], joined[rows:]
    for mask in masks:
        bit = (me // mask) % 2
        got = lax.ppermute(buf, "col", xor_pairs(ways, mask))
        held = buf.shape[0]
        out = jnp.zeros((2 * held,) + buf.shape[1:], buf.dtype)
        out = lax.dynamic_update_slice_in_dim(out, buf, bit * held, 0)
        out = lax.dynamic_update_slice_in_dim(out, got, (1 - bit) * held, 0)
        buf = out
    return buf, extra


def route_plan(table):
    size = lax.axis_size("row")
    n = size.bit_length() - 1
    masks = [1 << (n - 1 - i) for i in range(n)]
    h = n // 2
    me = lax.axis_index("row")
    high = sum(masks[:h])
    wide = 1 << (n - h)
    j = jnp.arange(wide, dtype=jnp.int32)
    dest = (me & high) + sum(((j >> i) & 1) * masks[h + i] for i in range(n - h))
    src = table[dest]
    slots = sum(((src // masks[i]) % 2) << i for i in range(h))
    conds = []
    for u in range(n - h):
        m = masks[h + u]
        k = jnp.arange(wide >> (u + 1), dtype=jnp.int32)
        done_bits = high + sum(masks[h:h + u + 1])
        kept = (me & done_bits) + sum(((k >> i) & 1) * masks[h + u + 1 + i] for i in range(n - h - u - 1))
        conds.append((table[kept] // m) % 2 == (me // m) % 2)
    return masks, h, slots, conds


def route_forward(x, plan):
    masks, h, slots, conds = plan
    size = lax.axis_size("row")
    me = lax.axis_index("row")
    held = x[None]
    for t in range(h):
        m = masks[t]
        got = lax.ppermute(held, "row", xor_pairs(size, m))
        first = (me // m) % 2 == 0
        held = jnp.where(first, jnp.concatenate([held, got], 0), jnp.concatenate([got, held], 0))
    d = jnp.take(held, slots, axis=0)
    for u, c in enumerate(conds):
        m = masks[h + u]
        first = (me // m) % 2 == 0
        pair = d.reshape((-1, 2) + d.shape[1:])
        keep = jnp.where(first, pair[:, 0], pair[:, 1])
        send = jnp.where(first, pair[:, 1], pair[:, 0])
        got = lax.ppermute(send, "row", xor_pairs(size, m))
        d = jnp.where(c.reshape((-1,) + (1,) * (d.ndim - 1)), keep, got)
    return d[0]


def route_backward(g, plan):
    masks, h, slots, conds = plan
    size = lax.axis_size("row")
    me = lax.axis_index("row")
    dbar = g[None]
    for u in reversed(range(len(conds))):
        m = masks[h + u]
        first = (me // m) % 2 == 0
        c = conds[u].reshape((-1,) + (1,) * (dbar.ndim - 1))
        kbar = jnp.where(c, dbar, 0.0)
        rbar = jnp.where(c, 0.0, dbar)
        sbar = lax.ppermute(rbar.astype(jnp.bfloat16), "row", xor_pairs(size, m)).astype(jnp.float32)
        pair = jnp.where(first, jnp.stack([kbar, sbar], 1), jnp.stack([sbar, kbar], 1))
        dbar = pair.reshape((-1,) + dbar.shape[1:])
    pick = (slots[:, None] == jnp.arange(1 << h, dtype=jnp.int32)[None, :]).astype(jnp.float32)
    hbar = jnp.sum(pick.reshape(pick.shape + (1,) * (dbar.ndim - 1)) * dbar[:, None], axis=0)
    for t in reversed(range(h)):
        m = masks[t]
        first = (me // m) % 2 == 0
        half = hbar.shape[0] // 2
        mine = jnp.where(first, hbar[:half], hbar[half:])
        other = jnp.where(first, hbar[half:], hbar[:half])
        hbar = mine + lax.ppermute(other.astype(jnp.bfloat16), "row", xor_pairs(size, m)).astype(jnp.float32)
    return hbar[0]


def embed(pre):
    return pre * lax.rsqrt(jnp.sum(pre * pre, axis=-1, keepdims=True) + 1e-06)


def body(
    node_feats,
    source_feats,
    nbr_blocks,
    nbr_count,
    adj_tiles,
    pos_index,
    noise_block_rows,
    w_self,
    w_neigh,
):
    rows = node_feats.shape[0]
    width = node_feats.shape[1]
    slots = adj_tiles.shape[1]
    highest = lax.Precision.HIGHEST
    nodes = rows * lax.axis_size("row") * lax.axis_size("col")
    scale_factor = 1.0 / softness_divisor
    valid = jnp.arange(slots, dtype=jnp.int32)[None, :] < nbr_count[:, None]
    tiles = adj_tiles * valid[:, :, None, None].astype(jnp.bfloat16)
    piece = lax.all_gather(source_feats, "col", axis=0, tiled=True)
    count = piece.shape[0] // BLOCK
    blocks = piece.reshape(count, BLOCK, width)
    indicator_matrix = (
        nbr_blocks[:, :, None] == jnp.arange(count, dtype=jnp.int32)[None, None, :]
    ).astype(jnp.bfloat16)
    selected = jnp.einsum(
        "bkc,cjd->bkjd", indicator_matrix, blocks, preferred_element_type=jnp.float32
    ).astype(jnp.bfloat16)
    summed = jnp.einsum("bkij,bkjd->bid", tiles, selected, preferred_element_type=jnp.float32)
    agg = summed.reshape(rows, width).astype(jnp.bfloat16)
    pre = jnp.dot(node_feats, w_self, preferred_element_type=jnp.float32) + jnp.dot(
        agg, w_neigh, preferred_element_type=jnp.float32
    )
    emb32, pull = jax.vjp(embed, pre)
    zeta_bf = emb32.astype(jnp.bfloat16)
    plan = route_plan(noise_block_rows)
    noise_emb = route_forward(zeta_bf[:NOISE], plan).astype(jnp.float32)
    zeta = zeta_bf.astype(jnp.float32)
    pairing = (pos_index[:, None] == jnp.arange(rows, dtype=jnp.int32)[None, :]).astype(jnp.float32)
    partner = jnp.dot(pairing.astype(jnp.bfloat16), zeta_bf, preferred_element_type=jnp.float32)
    s_pos = jnp.sum(zeta * partner, axis=-1) * scale_factor
    s_neg = jnp.dot(zeta_bf, noise_emb.astype(jnp.bfloat16).T, preferred_element_type=jnp.float32) * scale_factor
    loss_part = (jnp.sum(jax.nn.softplus(-s_pos)) + jnp.sum(jax.nn.softplus(s_neg)) / NOISE) / nodes
    grad_pos = -jax.nn.sigmoid(-s_pos) / nodes
    grad_neg = jax.nn.sigmoid(s_neg) / (NOISE * nodes)
    anchor = scale_factor * (
        grad_pos[:, None] * partner + jnp.dot(grad_neg, noise_emb, precision=highest)
    )
    partner_grad = jnp.dot(pairing.T, scale_factor * grad_pos[:, None] * zeta, precision=highest)
    dnoise = scale_factor * jnp.dot(grad_neg.T, zeta, precision=highest)
    returned = route_backward(dnoise.astype(jnp.bfloat16).astype(jnp.float32), plan)
    dzeta = anchor + partner_grad
    dzeta = dzeta.at[:NOISE].add(returned)
    gpre = pull(dzeta)[0].astype(jnp.bfloat16)
    part_self = jnp.dot(node_feats.T, gpre, preferred_element_type=jnp.float32)
    neighbour_partial = jnp.dot(agg.T, gpre, preferred_element_type=jnp.float32)
    stacked = jnp.concatenate([part_self, neighbour_partial], axis=0)
    total, loss_tile = tree_allreduce(stacked, jnp.broadcast_to(loss_part, (8, width)))
    grad_self = total[:width]
    neighbour_weight_gradient = total[width:]
    return (grad_self, neighbour_weight_gradient, loss_tile[0, 0])


def solution(mesh):
    in_specs = (
        P(("row", "col"), None),
        P("col", None),
        P(("row", "col"), None),
        P(("row", "col")),
        P(("row", "col"), None, None, None),
        P(("row", "col")),
        P(),
        P(),
        P(),
    )
    out_specs = (P(), P(), P())
    return jax.shard_map(body, mesh=mesh, in_specs=in_specs, out_specs=out_specs, check_vma=False)
```

```python
import jax
import jax.numpy as jnp
from jax import lax
from jax.sharding import PartitionSpec as P

BLOCK = 128
NOISE = 128


softness_divisor = 0.2


def xor_pairs(size, mask):
    return [(i, i ^ mask) for i in range(size)]


DOUBLING = (("col", 16), ("col", 8), ("col", 4), ("col", 2), ("col", 1))
BUTTERFLY = (("row", 1), ("row", 2), ("row", 4), ("row", 8))


def tree_allreduce(buf, extra):
    ways = lax.axis_size("col")
    me = lax.axis_index("col")
    masks = [mask for axis, mask in DOUBLING if mask < ways]
    position = [sum(((j // mask) % 2) << t for t, mask in enumerate(masks)) for j in range(ways)]
    rows = buf.shape[0] // ways
    chunks = buf.reshape(ways, rows, buf.shape[1])[jnp.array(position, jnp.int32)]
    chunks = jnp.concatenate([chunks, jnp.broadcast_to(extra[None], (ways,) + extra.shape)], axis=1)
    joined = lax.all_to_all(chunks, "col", 0, 0, tiled=False).sum(axis=0)
    for axis, mask in BUTTERFLY:
        size = lax.axis_size(axis)
        if mask >= size:
            continue
        joined = joined + lax.ppermute(joined, axis, xor_pairs(size, mask))
    buf, extra = joined[:rows], joined[rows:]
    for mask in masks:
        bit = (me // mask) % 2
        got = lax.ppermute(buf, "col", xor_pairs(ways, mask))
        held = buf.shape[0]
        out = jnp.zeros((2 * held,) + buf.shape[1:], buf.dtype)
        out = lax.dynamic_update_slice_in_dim(out, buf, bit * held, 0)
        out = lax.dynamic_update_slice_in_dim(out, got, (1 - bit) * held, 0)
        buf = out
    return buf, extra


def route_plan(table):
    size = lax.axis_size("row")
    n = size.bit_length() - 1
    masks = [1 << (n - 1)] + [1 << i for i in range(n - 1)]
    h = n // 2
    me = lax.axis_index("row")
    high = sum(masks[:h])
    wide = 1 << (n - h)
    j = jnp.arange(wide, dtype=jnp.int32)
    dest = (me & high) + sum(((j >> i) & 1) * masks[h + i] for i in range(n - h))
    src = table[dest]
    slots = sum(((src // masks[i]) % 2) << i for i in range(h))
    conds = []
    for u in range(n - h):
        m = masks[h + u]
        k = jnp.arange(wide >> (u + 1), dtype=jnp.int32)
        done_bits = high + sum(masks[h:h + u + 1])
        kept = (me & done_bits) + sum(((k >> i) & 1) * masks[h + u + 1 + i] for i in range(n - h - u - 1))
        conds.append((table[kept] // m) % 2 == (me // m) % 2)
    return masks, h, slots, conds


def route_forward(x, plan):
    masks, h, slots, conds = plan
    size = lax.axis_size("row")
    me = lax.axis_index("row")
    held = x[None]
    for t in range(h):
        m = masks[t]
        got = lax.ppermute(held, "row", xor_pairs(size, m))
        first = (me // m) % 2 == 0
        held = jnp.where(first, jnp.concatenate([held, got], 0), jnp.concatenate([got, held], 0))
    d = jnp.take(held, slots, axis=0)
    for u, c in enumerate(conds):
        m = masks[h + u]
        first = (me // m) % 2 == 0
        pair = d.reshape((-1, 2) + d.shape[1:])
        keep = jnp.where(first, pair[:, 0], pair[:, 1])
        send = jnp.where(first, pair[:, 1], pair[:, 0])
        got = lax.ppermute(send, "row", xor_pairs(size, m))
        d = jnp.where(c.reshape((-1,) + (1,) * (d.ndim - 1)), keep, got)
    return d[0]


def route_backward(g, plan):
    masks, h, slots, conds = plan
    size = lax.axis_size("row")
    me = lax.axis_index("row")
    dbar = g[None]
    for u in reversed(range(len(conds))):
        m = masks[h + u]
        first = (me // m) % 2 == 0
        c = conds[u].reshape((-1,) + (1,) * (dbar.ndim - 1))
        kbar = jnp.where(c, dbar, 0.0)
        rbar = jnp.where(c, 0.0, dbar)
        sbar = lax.ppermute(rbar.astype(jnp.bfloat16), "row", xor_pairs(size, m)).astype(jnp.float32)
        pair = jnp.where(first, jnp.stack([kbar, sbar], 1), jnp.stack([sbar, kbar], 1))
        dbar = pair.reshape((-1,) + dbar.shape[1:])
    pick = (slots[:, None] == jnp.arange(1 << h, dtype=jnp.int32)[None, :]).astype(jnp.float32)
    hbar = jnp.sum(pick.reshape(pick.shape + (1,) * (dbar.ndim - 1)) * dbar[:, None], axis=0)
    for t in reversed(range(h)):
        m = masks[t]
        first = (me // m) % 2 == 0
        half = hbar.shape[0] // 2
        mine = jnp.where(first, hbar[:half], hbar[half:])
        other = jnp.where(first, hbar[half:], hbar[:half])
        hbar = mine + lax.ppermute(other.astype(jnp.bfloat16), "row", xor_pairs(size, m)).astype(jnp.float32)
    return hbar[0]


def embed(pre):
    return pre * lax.rsqrt(jnp.sum(pre * pre, axis=-1, keepdims=True) + 1e-06)


def body(
    node_feats,
    source_feats,
    nbr_blocks,
    nbr_count,
    adj_tiles,
    pos_index,
    noise_block_rows,
    w_self,
    w_neigh,
):
    rows = node_feats.shape[0]
    width = node_feats.shape[1]
    slots = adj_tiles.shape[1]
    highest = lax.Precision.HIGHEST
    nodes = rows * lax.axis_size("row") * lax.axis_size("col")
    scale_factor = 1.0 / softness_divisor
    valid = jnp.arange(slots, dtype=jnp.int32)[None, :] < nbr_count[:, None]
    tiles = adj_tiles * valid[:, :, None, None].astype(jnp.bfloat16)
    piece = lax.all_gather(source_feats, "col", axis=0, tiled=True)
    count = piece.shape[0] // BLOCK
    blocks = piece.reshape(count, BLOCK, width)
    indicator_matrix = (
        nbr_blocks[:, :, None] == jnp.arange(count, dtype=jnp.int32)[None, None, :]
    ).astype(jnp.bfloat16)
    selected = jnp.einsum(
        "bkc,cjd->bkjd", indicator_matrix, blocks, preferred_element_type=jnp.float32
    ).astype(jnp.bfloat16)
    summed = jnp.einsum("bkij,bkjd->bid", tiles, selected, preferred_element_type=jnp.float32)
    agg = summed.reshape(rows, width).astype(jnp.bfloat16)
    pre = jnp.dot(node_feats, w_self, preferred_element_type=jnp.float32) + jnp.dot(
        agg, w_neigh, preferred_element_type=jnp.float32
    )
    emb32, pull = jax.vjp(embed, pre)
    zeta_bf = emb32.astype(jnp.bfloat16)
    plan = route_plan(noise_block_rows)
    noise_emb = route_forward(zeta_bf[:NOISE], plan).astype(jnp.float32)
    zeta = zeta_bf.astype(jnp.float32)
    pairing = (pos_index[:, None] == jnp.arange(rows, dtype=jnp.int32)[None, :]).astype(jnp.float32)
    partner = jnp.dot(pairing.astype(jnp.bfloat16), zeta_bf, preferred_element_type=jnp.float32)
    s_pos = jnp.sum(zeta * partner, axis=-1) * scale_factor
    s_neg = jnp.dot(zeta_bf, noise_emb.astype(jnp.bfloat16).T, preferred_element_type=jnp.float32) * scale_factor
    loss_part = (jnp.sum(jax.nn.softplus(-s_pos)) + jnp.sum(jax.nn.softplus(s_neg)) / NOISE) / nodes
    grad_pos = -jax.nn.sigmoid(-s_pos) / nodes
    grad_neg = jax.nn.sigmoid(s_neg) / (NOISE * nodes)
    anchor = scale_factor * (
        grad_pos[:, None] * partner + jnp.dot(grad_neg, noise_emb, precision=highest)
    )
    partner_grad = jnp.dot(pairing.T, scale_factor * grad_pos[:, None] * zeta, precision=highest)
    dnoise = scale_factor * jnp.dot(grad_neg.T, zeta, precision=highest)
    returned = route_backward(dnoise.astype(jnp.bfloat16).astype(jnp.float32), plan)
    dzeta = anchor + partner_grad
    dzeta = dzeta.at[:NOISE].add(returned)
    gpre = pull(dzeta)[0].astype(jnp.bfloat16)
    part_self = jnp.dot(node_feats.T, gpre, preferred_element_type=jnp.float32)
    neighbour_partial = jnp.dot(agg.T, gpre, preferred_element_type=jnp.float32)
    stacked = jnp.concatenate([part_self, neighbour_partial], axis=0)
    total, loss_tile = tree_allreduce(stacked, jnp.broadcast_to(loss_part, (8, width)))
    grad_self = total[:width]
    neighbour_weight_gradient = total[width:]
    return (grad_self, neighbour_weight_gradient, loss_tile[0, 0])


def solution(mesh):
    in_specs = (
        P(("row", "col"), None),
        P("col", None),
        P(("row", "col"), None),
        P(("row", "col")),
        P(("row", "col"), None, None, None),
        P(("row", "col")),
        P(),
        P(),
        P(),
    )
    out_specs = (P(), P(), P())
    return jax.shard_map(body, mesh=mesh, in_specs=in_specs, out_specs=out_specs, check_vma=False)
```

```python
import jax
import jax.numpy as jnp
from jax import lax
from jax.sharding import PartitionSpec as P

BLOCK = 128
NOISE = 128


softness_divisor = 0.2


def xor_pairs(size, mask):
    return [(i, i ^ mask) for i in range(size)]


DOUBLING = (("col", 16), ("col", 8), ("col", 4), ("col", 2), ("col", 1))
BUTTERFLY = (("row", 1), ("row", 2), ("row", 4), ("row", 8))


def tree_allreduce(buf, extra):
    ways = lax.axis_size("col")
    me = lax.axis_index("col")
    masks = [mask for axis, mask in DOUBLING if mask < ways]
    position = [sum(((j // mask) % 2) << t for t, mask in enumerate(masks)) for j in range(ways)]
    rows = buf.shape[0] // ways
    chunks = buf.reshape(ways, rows, buf.shape[1])[jnp.array(position, jnp.int32)]
    chunks = jnp.concatenate([chunks, jnp.broadcast_to(extra[None], (ways,) + extra.shape)], axis=1)
    joined = lax.all_to_all(chunks, "col", 0, 0, tiled=False).sum(axis=0)
    for axis, mask in BUTTERFLY:
        size = lax.axis_size(axis)
        if mask >= size:
            continue
        joined = joined + lax.ppermute(joined, axis, xor_pairs(size, mask))
    buf, extra = joined[:rows], joined[rows:]
    for mask in masks:
        bit = (me // mask) % 2
        got = lax.ppermute(buf, "col", xor_pairs(ways, mask))
        held = buf.shape[0]
        out = jnp.zeros((2 * held,) + buf.shape[1:], buf.dtype)
        out = lax.dynamic_update_slice_in_dim(out, buf, bit * held, 0)
        out = lax.dynamic_update_slice_in_dim(out, got, (1 - bit) * held, 0)
        buf = out
    return buf, extra


def route_plan(table):
    size = lax.axis_size("row")
    n = size.bit_length() - 1
    masks = [1 << (n - 1)] + [1 << i for i in range(n - 1)]
    h = n // 2
    me = lax.axis_index("row")
    high = sum(masks[:h])
    wide = 1 << (n - h)
    j = jnp.arange(wide, dtype=jnp.int32)
    dest = (me & high) + sum(((j >> i) & 1) * masks[h + i] for i in range(n - h))
    src = table[dest]
    slots = sum(((src // masks[i]) % 2) << i for i in range(h))
    conds = []
    for u in range(n - h):
        m = masks[h + u]
        k = jnp.arange(wide >> (u + 1), dtype=jnp.int32)
        done_bits = high + sum(masks[h:h + u + 1])
        kept = (me & done_bits) + sum(((k >> i) & 1) * masks[h + u + 1 + i] for i in range(n - h - u - 1))
        conds.append((table[kept] // m) % 2 == (me // m) % 2)
    return masks, h, slots, conds


def route_forward(x, plan):
    masks, h, slots, conds = plan
    size = lax.axis_size("row")
    me = lax.axis_index("row")
    held = x[None]
    for t in range(h):
        m = masks[t]
        got = lax.ppermute(held, "row", xor_pairs(size, m))
        first = (me // m) % 2 == 0
        held = jnp.where(first, jnp.concatenate([held, got], 0), jnp.concatenate([got, held], 0))
    d = jnp.take(held, slots, axis=0)
    for u, c in enumerate(conds):
        m = masks[h + u]
        first = (me // m) % 2 == 0
        pair = d.reshape((-1, 2) + d.shape[1:])
        keep = jnp.where(first, pair[:, 0], pair[:, 1])
        send = jnp.where(first, pair[:, 1], pair[:, 0])
        got = lax.ppermute(send, "row", xor_pairs(size, m))
        d = jnp.where(c.reshape((-1,) + (1,) * (d.ndim - 1)), keep, got)
    return d[0]


def route_backward(g, plan):
    masks, h, slots, conds = plan
    size = lax.axis_size("row")
    me = lax.axis_index("row")
    dbar = g[None]
    for u in reversed(range(len(conds))):
        m = masks[h + u]
        first = (me // m) % 2 == 0
        c = conds[u].reshape((-1,) + (1,) * (dbar.ndim - 1))
        kbar = jnp.where(c, dbar, 0.0)
        rbar = jnp.where(c, 0.0, dbar)
        sbar = lax.ppermute(rbar.astype(jnp.bfloat16), "row", xor_pairs(size, m)).astype(jnp.float32)
        pair = jnp.where(first, jnp.stack([kbar, sbar], 1), jnp.stack([sbar, kbar], 1))
        dbar = pair.reshape((-1,) + dbar.shape[1:])
    pick = (slots[:, None] == jnp.arange(1 << h, dtype=jnp.int32)[None, :]).astype(jnp.float32)
    hbar = jnp.sum(pick.reshape(pick.shape + (1,) * (dbar.ndim - 1)) * dbar[:, None], axis=0)
    for t in reversed(range(h)):
        m = masks[t]
        first = (me // m) % 2 == 0
        half = hbar.shape[0] // 2
        mine = jnp.where(first, hbar[:half], hbar[half:])
        other = jnp.where(first, hbar[half:], hbar[:half])
        hbar = mine + lax.ppermute(other.astype(jnp.bfloat16), "row", xor_pairs(size, m)).astype(jnp.float32)
    return hbar[0]


def embed(pre):
    return pre * lax.rsqrt(jnp.sum(pre * pre, axis=-1, keepdims=True) + 1e-06)


def body(
    node_feats,
    source_feats,
    nbr_blocks,
    nbr_count,
    adj_tiles,
    pos_index,
    noise_block_rows,
    w_self,
    w_neigh,
):
    rows = node_feats.shape[0]
    width = node_feats.shape[1]
    slots = adj_tiles.shape[1]
    highest = lax.Precision.HIGHEST
    nodes = rows * lax.axis_size("row") * lax.axis_size("col")
    scale_factor = 1.0 / softness_divisor
    valid = jnp.arange(slots, dtype=jnp.int32)[None, :] < nbr_count[:, None]
    tiles = adj_tiles * valid[:, :, None, None].astype(jnp.bfloat16)
    piece = lax.all_gather(source_feats, "col", axis=0, tiled=True)
    count = piece.shape[0] // BLOCK
    blocks = piece.reshape(count, BLOCK, width)
    indicator_matrix = (
        nbr_blocks[:, :, None] == jnp.arange(count, dtype=jnp.int32)[None, None, :]
    ).astype(jnp.bfloat16)
    selected = jnp.einsum(
        "bkc,cjd->bkjd", indicator_matrix, blocks, preferred_element_type=jnp.float32
    ).astype(jnp.bfloat16)
    summed = jnp.einsum("bkij,bkjd->bid", tiles, selected, preferred_element_type=jnp.float32)
    agg = summed.reshape(rows, width).astype(jnp.bfloat16)
    plan = route_plan(noise_block_rows)
    fetched = route_forward(jnp.concatenate([node_feats[:NOISE], agg[:NOISE]], axis=0), plan)
    all_feats = jnp.concatenate([node_feats, fetched[:NOISE]], axis=0)
    all_agg = jnp.concatenate([agg, fetched[NOISE:]], axis=0)
    pre = jnp.dot(all_feats, w_self, preferred_element_type=jnp.float32) + jnp.dot(
        all_agg, w_neigh, preferred_element_type=jnp.float32
    )
    emb32, pull = jax.vjp(embed, pre)
    all_bf = emb32.astype(jnp.bfloat16)
    zeta_bf = all_bf[:rows]
    noise_emb = all_bf[rows:].astype(jnp.float32)
    zeta = zeta_bf.astype(jnp.float32)
    pairing = (pos_index[:, None] == jnp.arange(rows, dtype=jnp.int32)[None, :]).astype(jnp.float32)
    partner = jnp.dot(pairing.astype(jnp.bfloat16), zeta_bf, preferred_element_type=jnp.float32)
    s_pos = jnp.sum(zeta * partner, axis=-1) * scale_factor
    s_neg = jnp.dot(zeta_bf, all_bf[rows:].T, preferred_element_type=jnp.float32) * scale_factor
    loss_part = (jnp.sum(jax.nn.softplus(-s_pos)) + jnp.sum(jax.nn.softplus(s_neg)) / NOISE) / nodes
    grad_pos = -jax.nn.sigmoid(-s_pos) / nodes
    grad_neg = jax.nn.sigmoid(s_neg) / (NOISE * nodes)
    anchor = scale_factor * (
        grad_pos[:, None] * partner + jnp.dot(grad_neg, noise_emb, precision=highest)
    )
    partner_grad = jnp.dot(pairing.T, scale_factor * grad_pos[:, None] * zeta, precision=highest)
    dnoise = scale_factor * jnp.dot(grad_neg.T, zeta, precision=highest)
    dnoise = dnoise.astype(jnp.bfloat16).astype(jnp.float32)
    dzeta = jnp.concatenate([anchor + partner_grad, dnoise], axis=0)
    gpre = pull(dzeta)[0].astype(jnp.bfloat16)
    part_self = jnp.dot(all_feats.T, gpre, preferred_element_type=jnp.float32)
    neighbour_partial = jnp.dot(all_agg.T, gpre, preferred_element_type=jnp.float32)
    stacked = jnp.concatenate([part_self, neighbour_partial], axis=0)
    total, loss_tile = tree_allreduce(stacked, jnp.broadcast_to(loss_part, (8, width)))
    grad_self = total[:width]
    neighbour_weight_gradient = total[width:]
    return (grad_self, neighbour_weight_gradient, loss_tile[0, 0])


def solution(mesh):
    in_specs = (
        P(("row", "col"), None),
        P("col", None),
        P(("row", "col"), None),
        P(("row", "col")),
        P(("row", "col"), None, None, None),
        P(("row", "col")),
        P(),
        P(),
        P(),
    )
    out_specs = (P(), P(), P())
    return jax.shard_map(body, mesh=mesh, in_specs=in_specs, out_specs=out_specs, check_vma=False)
```

```python
import jax
import jax.numpy as jnp
from jax import lax
from jax.sharding import PartitionSpec as P

BLOCK = 128
NOISE = 128


softness_divisor = 0.2


def xor_pairs(size, mask):
    return [(i, i ^ mask) for i in range(size)]


DOUBLING = (("col", 16), ("col", 8), ("col", 4), ("col", 2), ("col", 1))
BUTTERFLY = (("row", 1), ("row", 2), ("row", 4), ("row", 8))


def tree_allreduce(buf, extra):
    ways = lax.axis_size("col")
    me = lax.axis_index("col")
    masks = [mask for axis, mask in DOUBLING if mask < ways]
    position = [sum(((j // mask) % 2) << t for t, mask in enumerate(masks)) for j in range(ways)]
    rows = buf.shape[0] // ways
    chunks = buf.reshape(ways, rows, buf.shape[1])[jnp.array(position, jnp.int32)]
    chunks = jnp.concatenate([chunks, jnp.broadcast_to(extra[None], (ways,) + extra.shape)], axis=1)
    joined = lax.all_to_all(chunks, "col", 0, 0, tiled=False).sum(axis=0)
    for axis, mask in BUTTERFLY:
        size = lax.axis_size(axis)
        if mask >= size:
            continue
        joined = joined + lax.ppermute(joined, axis, xor_pairs(size, mask))
    buf, extra = joined[:rows], joined[rows:]
    for mask in masks:
        bit = (me // mask) % 2
        got = lax.ppermute(buf, "col", xor_pairs(ways, mask))
        held = buf.shape[0]
        out = jnp.zeros((2 * held,) + buf.shape[1:], buf.dtype)
        out = lax.dynamic_update_slice_in_dim(out, buf, bit * held, 0)
        out = lax.dynamic_update_slice_in_dim(out, got, (1 - bit) * held, 0)
        buf = out
    return buf, extra


def route_plan(table):
    size = lax.axis_size("row")
    n = size.bit_length() - 1
    masks = [1 << (n - 1)] + [1 << i for i in range(n - 1)]
    h = n // 2
    me = lax.axis_index("row")
    high = sum(masks[:h])
    wide = 1 << (n - h)
    j = jnp.arange(wide, dtype=jnp.int32)
    dest = (me & high) + sum(((j >> i) & 1) * masks[h + i] for i in range(n - h))
    src = table[dest]
    slots = sum(((src // masks[i]) % 2) << i for i in range(h))
    conds = []
    for u in range(n - h):
        m = masks[h + u]
        k = jnp.arange(wide >> (u + 1), dtype=jnp.int32)
        done_bits = high + sum(masks[h:h + u + 1])
        kept = (me & done_bits) + sum(((k >> i) & 1) * masks[h + u + 1 + i] for i in range(n - h - u - 1))
        conds.append((table[kept] // m) % 2 == (me // m) % 2)
    return masks, h, slots, conds


def route_forward(x, plan):
    masks, h, slots, conds = plan
    size = lax.axis_size("row")
    me = lax.axis_index("row")
    held = x[None]
    for t in range(h):
        m = masks[t]
        got = lax.ppermute(held, "row", xor_pairs(size, m))
        first = (me // m) % 2 == 0
        held = jnp.where(first, jnp.concatenate([held, got], 0), jnp.concatenate([got, held], 0))
    d = jnp.take(held, slots, axis=0)
    for u, c in enumerate(conds):
        m = masks[h + u]
        first = (me // m) % 2 == 0
        pair = d.reshape((-1, 2) + d.shape[1:])
        keep = jnp.where(first, pair[:, 0], pair[:, 1])
        send = jnp.where(first, pair[:, 1], pair[:, 0])
        got = lax.ppermute(send, "row", xor_pairs(size, m))
        d = jnp.where(c.reshape((-1,) + (1,) * (d.ndim - 1)), keep, got)
    return d[0]


def route_backward(g, plan):
    masks, h, slots, conds = plan
    size = lax.axis_size("row")
    me = lax.axis_index("row")
    dbar = g[None]
    for u in reversed(range(len(conds))):
        m = masks[h + u]
        first = (me // m) % 2 == 0
        c = conds[u].reshape((-1,) + (1,) * (dbar.ndim - 1))
        kbar = jnp.where(c, dbar, 0.0)
        rbar = jnp.where(c, 0.0, dbar)
        sbar = lax.ppermute(rbar.astype(jnp.bfloat16), "row", xor_pairs(size, m)).astype(jnp.float32)
        pair = jnp.where(first, jnp.stack([kbar, sbar], 1), jnp.stack([sbar, kbar], 1))
        dbar = pair.reshape((-1,) + dbar.shape[1:])
    pick = (slots[:, None] == jnp.arange(1 << h, dtype=jnp.int32)[None, :]).astype(jnp.float32)
    hbar = jnp.sum(pick.reshape(pick.shape + (1,) * (dbar.ndim - 1)) * dbar[:, None], axis=0)
    for t in reversed(range(h)):
        m = masks[t]
        first = (me // m) % 2 == 0
        half = hbar.shape[0] // 2
        mine = jnp.where(first, hbar[:half], hbar[half:])
        other = jnp.where(first, hbar[half:], hbar[:half])
        hbar = mine + lax.ppermute(other.astype(jnp.bfloat16), "row", xor_pairs(size, m)).astype(jnp.float32)
    return hbar[0]


def embed(pre):
    return pre * lax.rsqrt(jnp.sum(pre * pre, axis=-1, keepdims=True) + 1e-06)


def body(
    node_feats,
    source_feats,
    nbr_blocks,
    nbr_count,
    adj_tiles,
    pos_index,
    noise_block_rows,
    w_self,
    w_neigh,
):
    rows = node_feats.shape[0]
    width = node_feats.shape[1]
    slots = adj_tiles.shape[1]
    highest = lax.Precision.HIGHEST
    nodes = rows * lax.axis_size("row") * lax.axis_size("col")
    scale_factor = 1.0 / softness_divisor
    valid = jnp.arange(slots, dtype=jnp.int32)[None, :] < nbr_count[:, None]
    tiles = adj_tiles * valid[:, :, None, None].astype(jnp.bfloat16)
    plan = route_plan(noise_block_rows)
    noise_feats = route_forward(node_feats[:NOISE], plan)
    piece = lax.all_gather(source_feats, "col", axis=0, tiled=True)
    piece, noise_feats = lax.optimization_barrier((piece, noise_feats))
    count = piece.shape[0] // BLOCK
    blocks = piece.reshape(count, BLOCK, width)

    def aggregate(part_tiles, part_ids):
        indicator_matrix = (
            part_ids[:, :, None] == jnp.arange(count, dtype=jnp.int32)[None, None, :]
        ).astype(jnp.bfloat16)
        selected = jnp.einsum(
            "bkc,cjd->bkjd", indicator_matrix, blocks, preferred_element_type=jnp.float32
        ).astype(jnp.bfloat16)
        summed = jnp.einsum("bkij,bkjd->bid", part_tiles, selected, preferred_element_type=jnp.float32)
        return summed.reshape(-1, width).astype(jnp.bfloat16)

    head = NOISE // BLOCK
    agg_head = aggregate(tiles[:head], nbr_blocks[:head])
    noise_agg = route_forward(agg_head, plan)
    agg = jnp.concatenate([agg_head, aggregate(tiles[head:], nbr_blocks[head:])], axis=0)
    all_feats = jnp.concatenate([node_feats, noise_feats], axis=0)
    all_agg = jnp.concatenate([agg, noise_agg], axis=0)
    pre = jnp.dot(all_feats, w_self, preferred_element_type=jnp.float32) + jnp.dot(
        all_agg, w_neigh, preferred_element_type=jnp.float32
    )
    emb32, pull = jax.vjp(embed, pre)
    all_bf = emb32.astype(jnp.bfloat16)
    zeta_bf = all_bf[:rows]
    noise_emb = all_bf[rows:].astype(jnp.float32)
    zeta = zeta_bf.astype(jnp.float32)
    pairing = (pos_index[:, None] == jnp.arange(rows, dtype=jnp.int32)[None, :]).astype(jnp.float32)
    partner = jnp.dot(pairing.astype(jnp.bfloat16), zeta_bf, preferred_element_type=jnp.float32)
    s_pos = jnp.sum(zeta * partner, axis=-1) * scale_factor
    s_neg = jnp.dot(zeta_bf, all_bf[rows:].T, preferred_element_type=jnp.float32) * scale_factor
    loss_part = (jnp.sum(jax.nn.softplus(-s_pos)) + jnp.sum(jax.nn.softplus(s_neg)) / NOISE) / nodes
    grad_pos = -jax.nn.sigmoid(-s_pos) / nodes
    grad_neg = jax.nn.sigmoid(s_neg) / (NOISE * nodes)
    anchor = scale_factor * (
        grad_pos[:, None] * partner + jnp.dot(grad_neg, noise_emb, precision=highest)
    )
    partner_grad = jnp.dot(pairing.T, scale_factor * grad_pos[:, None] * zeta, precision=highest)
    dnoise = scale_factor * jnp.dot(grad_neg.T, zeta, precision=highest)
    dnoise = dnoise.astype(jnp.bfloat16).astype(jnp.float32)
    dzeta = jnp.concatenate([anchor + partner_grad, dnoise], axis=0)
    gpre = pull(dzeta)[0].astype(jnp.bfloat16)
    part_self = jnp.dot(all_feats.T, gpre, preferred_element_type=jnp.float32)
    neighbour_partial = jnp.dot(all_agg.T, gpre, preferred_element_type=jnp.float32)
    stacked = jnp.concatenate([part_self, neighbour_partial], axis=0)
    total, loss_tile = tree_allreduce(stacked, jnp.broadcast_to(loss_part, (8, width)))
    grad_self = total[:width]
    neighbour_weight_gradient = total[width:]
    return (grad_self, neighbour_weight_gradient, loss_tile[0, 0])


def solution(mesh):
    in_specs = (
        P(("row", "col"), None),
        P("col", None),
        P(("row", "col"), None),
        P(("row", "col")),
        P(("row", "col"), None, None, None),
        P(("row", "col")),
        P(),
        P(),
        P(),
    )
    out_specs = (P(), P(), P())
    return jax.shard_map(body, mesh=mesh, in_specs=in_specs, out_specs=out_specs, check_vma=False)
```

```python
import jax
import jax.numpy as jnp
from jax import lax
from jax.sharding import PartitionSpec as P

BLOCK = 128
NOISE = 128


softness_divisor = 0.2


def xor_pairs(size, mask):
    return [(i, i ^ mask) for i in range(size)]


DOUBLING = (("col", 16), ("col", 8), ("col", 4), ("col", 2), ("col", 1))
BUTTERFLY = (("row", 1), ("row", 2), ("row", 4), ("row", 8))


def tree_allreduce(buf, extra):
    ways = lax.axis_size("col")
    me = lax.axis_index("col")
    masks = [mask for axis, mask in DOUBLING if mask < ways]
    position = [sum(((j // mask) % 2) << t for t, mask in enumerate(masks)) for j in range(ways)]
    rows = buf.shape[0] // ways
    chunks = buf.reshape(ways, rows, buf.shape[1])[jnp.array(position, jnp.int32)]
    scattered = lax.all_to_all(chunks, "col", 0, 0, tiled=False).sum(axis=0)
    joined = jnp.concatenate([scattered, extra], axis=0)
    for axis, mask in BUTTERFLY:
        size = lax.axis_size(axis)
        if mask >= size:
            continue
        joined = joined + lax.ppermute(joined, axis, xor_pairs(size, mask))
    buf, extra = joined[:rows], joined[rows:]
    for mask in masks:
        bit = (me // mask) % 2
        held = buf.shape[0]
        got = lax.ppermute(jnp.concatenate([buf, extra], axis=0), "col", xor_pairs(ways, mask))
        extra = extra + got[held:]
        out = jnp.zeros((2 * held,) + buf.shape[1:], buf.dtype)
        out = lax.dynamic_update_slice_in_dim(out, buf, bit * held, 0)
        out = lax.dynamic_update_slice_in_dim(out, got[:held], (1 - bit) * held, 0)
        buf = out
    return buf, extra


def route_plan(table):
    size = lax.axis_size("row")
    n = size.bit_length() - 1
    masks = [1 << (n - 1)] + [1 << i for i in range(n - 1)]
    h = n // 2
    me = lax.axis_index("row")
    high = sum(masks[:h])
    wide = 1 << (n - h)
    j = jnp.arange(wide, dtype=jnp.int32)
    dest = (me & high) + sum(((j >> i) & 1) * masks[h + i] for i in range(n - h))
    src = table[dest]
    slots = sum(((src // masks[i]) % 2) << i for i in range(h))
    conds = []
    for u in range(n - h):
        m = masks[h + u]
        k = jnp.arange(wide >> (u + 1), dtype=jnp.int32)
        done_bits = high + sum(masks[h:h + u + 1])
        kept = (me & done_bits) + sum(((k >> i) & 1) * masks[h + u + 1 + i] for i in range(n - h - u - 1))
        conds.append((table[kept] // m) % 2 == (me // m) % 2)
    return masks, h, slots, conds


def route_forward(x, plan):
    masks, h, slots, conds = plan
    size = lax.axis_size("row")
    me = lax.axis_index("row")
    held = x[None]
    for t in range(h):
        m = masks[t]
        got = lax.ppermute(held, "row", xor_pairs(size, m))
        first = (me // m) % 2 == 0
        held = jnp.where(first, jnp.concatenate([held, got], 0), jnp.concatenate([got, held], 0))
    d = jnp.take(held, slots, axis=0)
    for u, c in enumerate(conds):
        m = masks[h + u]
        first = (me // m) % 2 == 0
        pair = d.reshape((-1, 2) + d.shape[1:])
        keep = jnp.where(first, pair[:, 0], pair[:, 1])
        send = jnp.where(first, pair[:, 1], pair[:, 0])
        got = lax.ppermute(send, "row", xor_pairs(size, m))
        d = jnp.where(c.reshape((-1,) + (1,) * (d.ndim - 1)), keep, got)
    return d[0]


def route_backward(g, plan):
    masks, h, slots, conds = plan
    size = lax.axis_size("row")
    me = lax.axis_index("row")
    dbar = g[None]
    for u in reversed(range(len(conds))):
        m = masks[h + u]
        first = (me // m) % 2 == 0
        c = conds[u].reshape((-1,) + (1,) * (dbar.ndim - 1))
        kbar = jnp.where(c, dbar, 0.0)
        rbar = jnp.where(c, 0.0, dbar)
        sbar = lax.ppermute(rbar.astype(jnp.bfloat16), "row", xor_pairs(size, m)).astype(jnp.float32)
        pair = jnp.where(first, jnp.stack([kbar, sbar], 1), jnp.stack([sbar, kbar], 1))
        dbar = pair.reshape((-1,) + dbar.shape[1:])
    pick = (slots[:, None] == jnp.arange(1 << h, dtype=jnp.int32)[None, :]).astype(jnp.float32)
    hbar = jnp.sum(pick.reshape(pick.shape + (1,) * (dbar.ndim - 1)) * dbar[:, None], axis=0)
    for t in reversed(range(h)):
        m = masks[t]
        first = (me // m) % 2 == 0
        half = hbar.shape[0] // 2
        mine = jnp.where(first, hbar[:half], hbar[half:])
        other = jnp.where(first, hbar[half:], hbar[:half])
        hbar = mine + lax.ppermute(other.astype(jnp.bfloat16), "row", xor_pairs(size, m)).astype(jnp.float32)
    return hbar[0]


def embed(pre):
    return pre * lax.rsqrt(jnp.sum(pre * pre, axis=-1, keepdims=True) + 1e-06)


def body(
    node_feats,
    source_feats,
    nbr_blocks,
    nbr_count,
    adj_tiles,
    pos_index,
    noise_block_rows,
    w_self,
    w_neigh,
):
    rows = node_feats.shape[0]
    width = node_feats.shape[1]
    slots = adj_tiles.shape[1]
    highest = lax.Precision.HIGHEST
    nodes = rows * lax.axis_size("row") * lax.axis_size("col")
    scale_factor = 1.0 / softness_divisor
    valid = jnp.arange(slots, dtype=jnp.int32)[None, :] < nbr_count[:, None]
    tiles = adj_tiles * valid[:, :, None, None].astype(jnp.bfloat16)
    plan = route_plan(noise_block_rows)
    noise_feats = route_forward(node_feats[:NOISE], plan)
    piece = lax.all_gather(source_feats, "col", axis=0, tiled=True)
    piece, noise_feats = lax.optimization_barrier((piece, noise_feats))
    count = piece.shape[0] // BLOCK
    blocks = piece.reshape(count, BLOCK, width)

    def aggregate(part_tiles, part_ids):
        indicator_matrix = (
            part_ids[:, :, None] == jnp.arange(count, dtype=jnp.int32)[None, None, :]
        ).astype(jnp.bfloat16)
        selected = jnp.einsum(
            "bkc,cjd->bkjd", indicator_matrix, blocks, preferred_element_type=jnp.float32
        ).astype(jnp.bfloat16)
        summed = jnp.einsum("bkij,bkjd->bid", part_tiles, selected, preferred_element_type=jnp.float32)
        return summed.reshape(-1, width).astype(jnp.bfloat16)

    head = NOISE // BLOCK
    agg_head = aggregate(tiles[:head], nbr_blocks[:head])
    noise_agg = route_forward(agg_head, plan)
    agg = jnp.concatenate([agg_head, aggregate(tiles[head:], nbr_blocks[head:])], axis=0)
    all_feats = jnp.concatenate([node_feats, noise_feats], axis=0)
    all_agg = jnp.concatenate([agg, noise_agg], axis=0)
    pre = jnp.dot(all_feats, w_self, preferred_element_type=jnp.float32) + jnp.dot(
        all_agg, w_neigh, preferred_element_type=jnp.float32
    )
    emb32, pull = jax.vjp(embed, pre)
    all_bf = emb32.astype(jnp.bfloat16)
    zeta_bf = all_bf[:rows]
    noise_emb = all_bf[rows:].astype(jnp.float32)
    zeta = zeta_bf.astype(jnp.float32)
    pairing = (pos_index[:, None] == jnp.arange(rows, dtype=jnp.int32)[None, :]).astype(jnp.float32)
    partner = jnp.dot(pairing.astype(jnp.bfloat16), zeta_bf, preferred_element_type=jnp.float32)
    s_pos = jnp.sum(zeta * partner, axis=-1) * scale_factor
    s_neg = jnp.dot(zeta_bf, all_bf[rows:].T, preferred_element_type=jnp.float32) * scale_factor
    loss_part = (jnp.sum(jax.nn.softplus(-s_pos)) + jnp.sum(jax.nn.softplus(s_neg)) / NOISE) / nodes
    grad_pos = -jax.nn.sigmoid(-s_pos) / nodes
    grad_neg = jax.nn.sigmoid(s_neg) / (NOISE * nodes)
    anchor = scale_factor * (
        grad_pos[:, None] * partner + jnp.dot(grad_neg, noise_emb, precision=highest)
    )
    partner_grad = jnp.dot(pairing.T, scale_factor * grad_pos[:, None] * zeta, precision=highest)
    dnoise = scale_factor * jnp.dot(grad_neg.T, zeta, precision=highest)
    dnoise = dnoise.astype(jnp.bfloat16).astype(jnp.float32)
    dzeta = jnp.concatenate([anchor + partner_grad, dnoise], axis=0)
    gpre = pull(dzeta)[0].astype(jnp.bfloat16)
    part_self = jnp.dot(all_feats.T, gpre, preferred_element_type=jnp.float32)
    neighbour_partial = jnp.dot(all_agg.T, gpre, preferred_element_type=jnp.float32)
    stacked = jnp.concatenate([part_self, neighbour_partial], axis=0)
    total, loss_tile = tree_allreduce(stacked, jnp.broadcast_to(loss_part, (8, width)))
    grad_self = total[:width]
    neighbour_weight_gradient = total[width:]
    return (grad_self, neighbour_weight_gradient, loss_tile[0, 0])


def solution(mesh):
    in_specs = (
        P(("row", "col"), None),
        P("col", None),
        P(("row", "col"), None),
        P(("row", "col")),
        P(("row", "col"), None, None, None),
        P(("row", "col")),
        P(),
        P(),
        P(),
    )
    out_specs = (P(), P(), P())
    return jax.shard_map(body, mesh=mesh, in_specs=in_specs, out_specs=out_specs, check_vma=False)
```

```python
import jax
import jax.numpy as jnp
from jax import lax
from jax.sharding import PartitionSpec as P

BLOCK = 128
NOISE = 128


softness_divisor = 0.2


def xor_pairs(size, mask):
    return [(i, i ^ mask) for i in range(size)]


DOUBLING = (("col", 16), ("col", 8), ("col", 4), ("col", 2), ("col", 1))
BUTTERFLY = (("row", 1), ("row", 2), ("row", 4), ("row", 8))


def tree_allreduce(buf, extra):
    ways = lax.axis_size("col")
    me = lax.axis_index("col")
    masks = [mask for axis, mask in DOUBLING if mask < ways]
    position = [sum(((j // mask) % 2) << t for t, mask in enumerate(masks)) for j in range(ways)]
    rows = buf.shape[0] // ways
    chunks = buf.reshape(ways, rows, buf.shape[1])[jnp.array(position, jnp.int32)]
    scattered = lax.all_to_all(chunks, "col", 0, 0, tiled=False).sum(axis=0)
    joined = jnp.concatenate([scattered, extra], axis=0)
    for axis, mask in BUTTERFLY:
        size = lax.axis_size(axis)
        if mask >= size:
            continue
        joined = joined + lax.ppermute(joined, axis, xor_pairs(size, mask))
    buf, extra = joined[:rows], joined[rows:]
    for mask in masks:
        bit = (me // mask) % 2
        held = buf.shape[0]
        got = lax.ppermute(jnp.concatenate([buf, extra], axis=0), "col", xor_pairs(ways, mask))
        extra = extra + got[held:]
        out = jnp.zeros((2 * held,) + buf.shape[1:], buf.dtype)
        out = lax.dynamic_update_slice_in_dim(out, buf, bit * held, 0)
        out = lax.dynamic_update_slice_in_dim(out, got[:held], (1 - bit) * held, 0)
        buf = out
    return buf, extra


def route_plan(table):
    size = lax.axis_size("row")
    n = size.bit_length() - 1
    masks = [1 << (n - 1)] + [1 << i for i in range(n - 1)]
    h = n // 2
    me = lax.axis_index("row")
    high = sum(masks[:h])
    wide = 1 << (n - h)
    j = jnp.arange(wide, dtype=jnp.int32)
    dest = (me & high) + sum(((j >> i) & 1) * masks[h + i] for i in range(n - h))
    src = table[dest]
    slots = sum(((src // masks[i]) % 2) << i for i in range(h))
    conds = []
    for u in range(n - h):
        m = masks[h + u]
        k = jnp.arange(wide >> (u + 1), dtype=jnp.int32)
        done_bits = high + sum(masks[h:h + u + 1])
        kept = (me & done_bits) + sum(((k >> i) & 1) * masks[h + u + 1 + i] for i in range(n - h - u - 1))
        conds.append((table[kept] // m) % 2 == (me // m) % 2)
    return masks, h, slots, conds


def route_forward(x, plan):
    masks, h, slots, conds = plan
    size = lax.axis_size("row")
    me = lax.axis_index("row")
    held = x[None]
    for t in range(h):
        m = masks[t]
        got = lax.ppermute(held, "row", xor_pairs(size, m))
        first = (me // m) % 2 == 0
        held = jnp.where(first, jnp.concatenate([held, got], 0), jnp.concatenate([got, held], 0))
    d = jnp.take(held, slots, axis=0)
    for u, c in enumerate(conds):
        m = masks[h + u]
        first = (me // m) % 2 == 0
        pair = d.reshape((-1, 2) + d.shape[1:])
        keep = jnp.where(first, pair[:, 0], pair[:, 1])
        send = jnp.where(first, pair[:, 1], pair[:, 0])
        got = lax.ppermute(send, "row", xor_pairs(size, m))
        d = jnp.where(c.reshape((-1,) + (1,) * (d.ndim - 1)), keep, got)
    return d[0]


def route_backward(g, plan):
    masks, h, slots, conds = plan
    size = lax.axis_size("row")
    me = lax.axis_index("row")
    dbar = g[None]
    for u in reversed(range(len(conds))):
        m = masks[h + u]
        first = (me // m) % 2 == 0
        c = conds[u].reshape((-1,) + (1,) * (dbar.ndim - 1))
        kbar = jnp.where(c, dbar, 0.0)
        rbar = jnp.where(c, 0.0, dbar)
        sbar = lax.ppermute(rbar.astype(jnp.bfloat16), "row", xor_pairs(size, m)).astype(jnp.float32)
        pair = jnp.where(first, jnp.stack([kbar, sbar], 1), jnp.stack([sbar, kbar], 1))
        dbar = pair.reshape((-1,) + dbar.shape[1:])
    pick = (slots[:, None] == jnp.arange(1 << h, dtype=jnp.int32)[None, :]).astype(jnp.float32)
    hbar = jnp.sum(pick.reshape(pick.shape + (1,) * (dbar.ndim - 1)) * dbar[:, None], axis=0)
    for t in reversed(range(h)):
        m = masks[t]
        first = (me // m) % 2 == 0
        half = hbar.shape[0] // 2
        mine = jnp.where(first, hbar[:half], hbar[half:])
        other = jnp.where(first, hbar[half:], hbar[:half])
        hbar = mine + lax.ppermute(other.astype(jnp.bfloat16), "row", xor_pairs(size, m)).astype(jnp.float32)
    return hbar[0]


def embed(pre):
    return pre * lax.rsqrt(jnp.sum(pre * pre, axis=-1, keepdims=True) + 1e-06)


def body(
    node_feats,
    source_feats,
    nbr_blocks,
    nbr_count,
    adj_tiles,
    pos_index,
    noise_block_rows,
    w_self,
    w_neigh,
):
    rows = node_feats.shape[0]
    width = node_feats.shape[1]
    slots = adj_tiles.shape[1]
    highest = lax.Precision.HIGHEST
    nodes = rows * lax.axis_size("row") * lax.axis_size("col")
    scale_factor = 1.0 / softness_divisor
    valid = jnp.arange(slots, dtype=jnp.int32)[None, :] < nbr_count[:, None]
    tiles = adj_tiles * valid[:, :, None, None].astype(jnp.bfloat16)
    plan = route_plan(noise_block_rows)
    noise_feats = route_forward(node_feats[:NOISE], plan)
    piece = lax.all_gather(source_feats, "col", axis=0, tiled=True)
    piece, noise_feats = lax.optimization_barrier((piece, noise_feats))
    count = piece.shape[0] // BLOCK
    blocks = piece.reshape(count, BLOCK, width)

    def aggregate(part_tiles, part_ids):
        selected = jnp.take(blocks, part_ids, axis=0, mode="clip")
        summed = jnp.einsum("bkij,bkjd->bid", part_tiles, selected, preferred_element_type=jnp.float32)
        return summed.reshape(-1, width).astype(jnp.bfloat16)

    head = NOISE // BLOCK
    agg_head = aggregate(tiles[:head], nbr_blocks[:head])
    noise_agg = route_forward(agg_head, plan)
    agg = jnp.concatenate([agg_head, aggregate(tiles[head:], nbr_blocks[head:])], axis=0)
    all_feats = jnp.concatenate([node_feats, noise_feats], axis=0)
    all_agg = jnp.concatenate([agg, noise_agg], axis=0)
    pre = jnp.dot(all_feats, w_self, preferred_element_type=jnp.float32) + jnp.dot(
        all_agg, w_neigh, preferred_element_type=jnp.float32
    )
    emb32, pull = jax.vjp(embed, pre)
    all_bf = emb32.astype(jnp.bfloat16)
    zeta_bf = all_bf[:rows]
    noise_emb = all_bf[rows:].astype(jnp.float32)
    zeta = zeta_bf.astype(jnp.float32)
    pairing = (pos_index[:, None] == jnp.arange(rows, dtype=jnp.int32)[None, :]).astype(jnp.float32)
    partner = jnp.dot(pairing.astype(jnp.bfloat16), zeta_bf, preferred_element_type=jnp.float32)
    s_pos = jnp.sum(zeta * partner, axis=-1) * scale_factor
    s_neg = jnp.dot(zeta_bf, all_bf[rows:].T, preferred_element_type=jnp.float32) * scale_factor
    loss_part = (jnp.sum(jax.nn.softplus(-s_pos)) + jnp.sum(jax.nn.softplus(s_neg)) / NOISE) / nodes
    grad_pos = -jax.nn.sigmoid(-s_pos) / nodes
    grad_neg = jax.nn.sigmoid(s_neg) / (NOISE * nodes)
    anchor = scale_factor * (
        grad_pos[:, None] * partner + jnp.dot(grad_neg, noise_emb, precision=highest)
    )
    partner_grad = jnp.dot(pairing.T, scale_factor * grad_pos[:, None] * zeta, precision=highest)
    dnoise = scale_factor * jnp.dot(grad_neg.T, zeta, precision=highest)
    dnoise = dnoise.astype(jnp.bfloat16).astype(jnp.float32)
    dzeta = jnp.concatenate([anchor + partner_grad, dnoise], axis=0)
    gpre = pull(dzeta)[0].astype(jnp.bfloat16)
    part_self = jnp.dot(all_feats.T, gpre, preferred_element_type=jnp.float32)
    neighbour_partial = jnp.dot(all_agg.T, gpre, preferred_element_type=jnp.float32)
    stacked = jnp.concatenate([part_self, neighbour_partial], axis=0)
    total, loss_tile = tree_allreduce(stacked, jnp.broadcast_to(loss_part, (8, width)))
    grad_self = total[:width]
    neighbour_weight_gradient = total[width:]
    return (grad_self, neighbour_weight_gradient, loss_tile[0, 0])


def solution(mesh):
    in_specs = (
        P(("row", "col"), None),
        P("col", None),
        P(("row", "col"), None),
        P(("row", "col")),
        P(("row", "col"), None, None, None),
        P(("row", "col")),
        P(),
        P(),
        P(),
    )
    out_specs = (P(), P(), P())
    return jax.shard_map(body, mesh=mesh, in_specs=in_specs, out_specs=out_specs, check_vma=False)
```

```python
import jax
import jax.numpy as jnp
from jax import lax
from jax.sharding import PartitionSpec as P

BLOCK = 128
NOISE = 128


softness_divisor = 0.2


def xor_pairs(size, mask):
    return [(i, i ^ mask) for i in range(size)]


DOUBLING = (("col", 16), ("col", 8), ("col", 4), ("col", 2), ("col", 1))
BUTTERFLY = (("row", 1), ("row", 2), ("row", 4), ("row", 8))


def tree_allreduce(buf, extra):
    ways = lax.axis_size("col")
    me = lax.axis_index("col")
    masks = [mask for axis, mask in DOUBLING if mask < ways]
    position = [sum(((j // mask) % 2) << t for t, mask in enumerate(masks)) for j in range(ways)]
    rows = buf.shape[0] // ways
    chunks = buf.reshape(ways, rows, buf.shape[1])[jnp.array(position, jnp.int32)]
    scattered = lax.all_to_all(chunks, "col", 0, 0, tiled=False).sum(axis=0)
    joined = jnp.concatenate([scattered, extra], axis=0)
    for axis, mask in BUTTERFLY:
        size = lax.axis_size(axis)
        if mask >= size:
            continue
        joined = joined + lax.ppermute(joined, axis, xor_pairs(size, mask))
    buf, extra = joined[:rows], joined[rows:]
    for mask in masks:
        bit = (me // mask) % 2
        held = buf.shape[0]
        got = lax.ppermute(jnp.concatenate([buf, extra], axis=0), "col", xor_pairs(ways, mask))
        extra = extra + got[held:]
        out = jnp.zeros((2 * held,) + buf.shape[1:], buf.dtype)
        out = lax.dynamic_update_slice_in_dim(out, buf, bit * held, 0)
        out = lax.dynamic_update_slice_in_dim(out, got[:held], (1 - bit) * held, 0)
        buf = out
    return buf, extra


def route_plan(table):
    size = lax.axis_size("row")
    n = size.bit_length() - 1
    masks = [1 << (n - 1)] + [1 << i for i in range(n - 1)]
    h = n // 2
    me = lax.axis_index("row")
    high = sum(masks[:h])
    wide = 1 << (n - h)
    j = jnp.arange(wide, dtype=jnp.int32)
    dest = (me & high) + sum(((j >> i) & 1) * masks[h + i] for i in range(n - h))
    src = table[dest]
    slots = sum(((src // masks[i]) % 2) << i for i in range(h))
    conds = []
    for u in range(n - h):
        m = masks[h + u]
        k = jnp.arange(wide >> (u + 1), dtype=jnp.int32)
        done_bits = high + sum(masks[h:h + u + 1])
        kept = (me & done_bits) + sum(((k >> i) & 1) * masks[h + u + 1 + i] for i in range(n - h - u - 1))
        conds.append((table[kept] // m) % 2 == (me // m) % 2)
    return masks, h, slots, conds


def route_forward(x, plan):
    masks, h, slots, conds = plan
    size = lax.axis_size("row")
    me = lax.axis_index("row")
    held = x[None]
    for t in range(h):
        m = masks[t]
        got = lax.ppermute(held, "row", xor_pairs(size, m))
        first = (me // m) % 2 == 0
        held = jnp.where(first, jnp.concatenate([held, got], 0), jnp.concatenate([got, held], 0))
    d = jnp.take(held, slots, axis=0)
    for u, c in enumerate(conds):
        m = masks[h + u]
        first = (me // m) % 2 == 0
        pair = d.reshape((-1, 2) + d.shape[1:])
        keep = jnp.where(first, pair[:, 0], pair[:, 1])
        send = jnp.where(first, pair[:, 1], pair[:, 0])
        got = lax.ppermute(send, "row", xor_pairs(size, m))
        d = jnp.where(c.reshape((-1,) + (1,) * (d.ndim - 1)), keep, got)
    return d[0]


def route_backward(g, plan):
    masks, h, slots, conds = plan
    size = lax.axis_size("row")
    me = lax.axis_index("row")
    dbar = g[None]
    for u in reversed(range(len(conds))):
        m = masks[h + u]
        first = (me // m) % 2 == 0
        c = conds[u].reshape((-1,) + (1,) * (dbar.ndim - 1))
        kbar = jnp.where(c, dbar, 0.0)
        rbar = jnp.where(c, 0.0, dbar)
        sbar = lax.ppermute(rbar.astype(jnp.bfloat16), "row", xor_pairs(size, m)).astype(jnp.float32)
        pair = jnp.where(first, jnp.stack([kbar, sbar], 1), jnp.stack([sbar, kbar], 1))
        dbar = pair.reshape((-1,) + dbar.shape[1:])
    pick = (slots[:, None] == jnp.arange(1 << h, dtype=jnp.int32)[None, :]).astype(jnp.float32)
    hbar = jnp.sum(pick.reshape(pick.shape + (1,) * (dbar.ndim - 1)) * dbar[:, None], axis=0)
    for t in reversed(range(h)):
        m = masks[t]
        first = (me // m) % 2 == 0
        half = hbar.shape[0] // 2
        mine = jnp.where(first, hbar[:half], hbar[half:])
        other = jnp.where(first, hbar[half:], hbar[:half])
        hbar = mine + lax.ppermute(other.astype(jnp.bfloat16), "row", xor_pairs(size, m)).astype(jnp.float32)
    return hbar[0]


def embed(pre):
    return pre * lax.rsqrt(jnp.sum(pre * pre, axis=-1, keepdims=True) + 1e-06)


def body(
    node_feats,
    source_feats,
    nbr_blocks,
    nbr_count,
    adj_tiles,
    pos_index,
    noise_block_rows,
    w_self,
    w_neigh,
):
    rows = node_feats.shape[0]
    width = node_feats.shape[1]
    slots = adj_tiles.shape[1]
    highest = lax.Precision.HIGHEST
    nodes = rows * lax.axis_size("row") * lax.axis_size("col")
    scale_factor = 1.0 / softness_divisor
    valid = jnp.arange(slots, dtype=jnp.int32)[None, :] < nbr_count[:, None]
    tiles = adj_tiles * valid[:, :, None, None].astype(jnp.bfloat16)
    plan = route_plan(noise_block_rows)
    noise_feats = route_forward(node_feats[:NOISE], plan)
    piece = lax.all_gather(source_feats, "col", axis=0, tiled=True)
    piece, noise_feats = lax.optimization_barrier((piece, noise_feats))
    count = piece.shape[0] // BLOCK
    blocks = piece.reshape(count, BLOCK, width)

    def aggregate(part_tiles, part_ids):
        selected = jnp.take(blocks, part_ids, axis=0, mode="clip")
        summed = jnp.einsum("bkij,bkjd->bid", part_tiles, selected, preferred_element_type=jnp.float32)
        return summed.reshape(-1, width).astype(jnp.bfloat16)

    head = NOISE // BLOCK
    agg_head = aggregate(tiles[:head], nbr_blocks[:head])
    noise_agg = route_forward(agg_head, plan)
    agg = jnp.concatenate([agg_head, aggregate(tiles[head:], nbr_blocks[head:])], axis=0)
    all_feats = jnp.concatenate([node_feats, noise_feats], axis=0)
    all_agg = jnp.concatenate([agg, noise_agg], axis=0)
    pre = jnp.dot(node_feats, w_self, preferred_element_type=jnp.float32) + jnp.dot(
        agg, w_neigh, preferred_element_type=jnp.float32
    )
    emb32, pull = jax.vjp(embed, pre)
    noise_pre = jnp.dot(noise_feats, w_self, preferred_element_type=jnp.float32) + jnp.dot(
        noise_agg, w_neigh, preferred_element_type=jnp.float32
    )
    noise_emb32, noise_pull = jax.vjp(embed, noise_pre)
    zeta_bf = emb32.astype(jnp.bfloat16)
    noise_bf = noise_emb32.astype(jnp.bfloat16)
    noise_emb = noise_bf.astype(jnp.float32)
    zeta = zeta_bf.astype(jnp.float32)
    pairing = (pos_index[:, None] == jnp.arange(rows, dtype=jnp.int32)[None, :]).astype(jnp.float32)
    partner = jnp.dot(pairing.astype(jnp.bfloat16), zeta_bf, preferred_element_type=jnp.float32)
    s_pos = jnp.sum(zeta * partner, axis=-1) * scale_factor
    s_neg = jnp.dot(zeta_bf, noise_bf.T, preferred_element_type=jnp.float32) * scale_factor
    loss_part = (jnp.sum(jax.nn.softplus(-s_pos)) + jnp.sum(jax.nn.softplus(s_neg)) / NOISE) / nodes
    grad_pos = -jax.nn.sigmoid(-s_pos) / nodes
    grad_neg = jax.nn.sigmoid(s_neg) / (NOISE * nodes)
    anchor = scale_factor * (
        grad_pos[:, None] * partner + jnp.dot(grad_neg, noise_emb, precision=highest)
    )
    partner_grad = jnp.dot(pairing.T, scale_factor * grad_pos[:, None] * zeta, precision=highest)
    dnoise = scale_factor * jnp.dot(grad_neg.T, zeta, precision=highest)
    dnoise = dnoise.astype(jnp.bfloat16).astype(jnp.float32)
    gpre = jnp.concatenate([pull(anchor + partner_grad)[0], noise_pull(dnoise)[0]], axis=0).astype(jnp.bfloat16)
    part_self = jnp.dot(all_feats.T, gpre, preferred_element_type=jnp.float32)
    neighbour_partial = jnp.dot(all_agg.T, gpre, preferred_element_type=jnp.float32)
    stacked = jnp.concatenate([part_self, neighbour_partial], axis=0)
    total, loss_tile = tree_allreduce(stacked, jnp.broadcast_to(loss_part, (8, width)))
    grad_self = total[:width]
    neighbour_weight_gradient = total[width:]
    return (grad_self, neighbour_weight_gradient, loss_tile[0, 0])


def solution(mesh):
    in_specs = (
        P(("row", "col"), None),
        P("col", None),
        P(("row", "col"), None),
        P(("row", "col")),
        P(("row", "col"), None, None, None),
        P(("row", "col")),
        P(),
        P(),
        P(),
    )
    out_specs = (P(), P(), P())
    return jax.shard_map(body, mesh=mesh, in_specs=in_specs, out_specs=out_specs, check_vma=False)
```

```python
import jax
import jax.numpy as jnp
from jax import lax
from jax.sharding import PartitionSpec as P

BLOCK = 128
NOISE = 128


softness_divisor = 0.2


def xor_pairs(size, mask):
    return [(i, i ^ mask) for i in range(size)]


DOUBLING = ((16, 8, 4, 2, 1), (4, 2, 16, 8, 1))
BUTTERFLY = (("row", 1), ("row", 2), ("row", 4), ("row", 8))


def tree_allreduce(buf, extra):
    ways = lax.axis_size("col")
    me = lax.axis_index("col")
    orders = [[mask for mask in order if mask < ways] for order in DOUBLING]
    position = [sum(((j // mask) % 2) << t for t, mask in enumerate(orders[j % 2])) for j in range(ways)]
    rows = buf.shape[0] // ways
    chunks = buf.reshape(ways, rows, buf.shape[1])[jnp.array(position, jnp.int32)]
    scattered = lax.all_to_all(chunks, "col", 0, 0, tiled=False).sum(axis=0)
    joined = jnp.concatenate([scattered, extra], axis=0)
    for axis, mask in BUTTERFLY:
        size = lax.axis_size(axis)
        if mask >= size:
            continue
        joined = joined + lax.ppermute(joined, axis, xor_pairs(size, mask))
    buf, extra = joined[:rows], joined[rows:]
    odd = me % 2 == 1
    for even_mask, odd_mask in zip(*orders):
        mask = jnp.where(odd, odd_mask, even_mask)
        bit = (me // mask) % 2
        held = buf.shape[0]
        pairs = [(i, i ^ (odd_mask if i % 2 else even_mask)) for i in range(ways)]
        got = lax.ppermute(jnp.concatenate([buf, extra], axis=0), "col", pairs)
        extra = extra + got[held:]
        out = jnp.zeros((2 * held,) + buf.shape[1:], buf.dtype)
        out = lax.dynamic_update_slice_in_dim(out, buf, bit * held, 0)
        out = lax.dynamic_update_slice_in_dim(out, got[:held], (1 - bit) * held, 0)
        buf = out
    return buf, extra


def route_plan(table):
    size = lax.axis_size("row")
    n = size.bit_length() - 1
    masks = [1 << (n - 1)] + [1 << i for i in range(n - 1)]
    h = n // 2
    me = lax.axis_index("row")
    high = sum(masks[:h])
    wide = 1 << (n - h)
    j = jnp.arange(wide, dtype=jnp.int32)
    dest = (me & high) + sum(((j >> i) & 1) * masks[h + i] for i in range(n - h))
    src = table[dest]
    slots = sum(((src // masks[i]) % 2) << i for i in range(h))
    conds = []
    for u in range(n - h):
        m = masks[h + u]
        k = jnp.arange(wide >> (u + 1), dtype=jnp.int32)
        done_bits = high + sum(masks[h:h + u + 1])
        kept = (me & done_bits) + sum(((k >> i) & 1) * masks[h + u + 1 + i] for i in range(n - h - u - 1))
        conds.append((table[kept] // m) % 2 == (me // m) % 2)
    return masks, h, slots, conds


def route_forward(x, plan):
    masks, h, slots, conds = plan
    size = lax.axis_size("row")
    me = lax.axis_index("row")
    held = x[None]
    for t in range(h):
        m = masks[t]
        got = lax.ppermute(held, "row", xor_pairs(size, m))
        first = (me // m) % 2 == 0
        held = jnp.where(first, jnp.concatenate([held, got], 0), jnp.concatenate([got, held], 0))
    d = jnp.take(held, slots, axis=0)
    for u, c in enumerate(conds):
        m = masks[h + u]
        first = (me // m) % 2 == 0
        pair = d.reshape((-1, 2) + d.shape[1:])
        keep = jnp.where(first, pair[:, 0], pair[:, 1])
        send = jnp.where(first, pair[:, 1], pair[:, 0])
        got = lax.ppermute(send, "row", xor_pairs(size, m))
        d = jnp.where(c.reshape((-1,) + (1,) * (d.ndim - 1)), keep, got)
    return d[0]


def route_backward(g, plan):
    masks, h, slots, conds = plan
    size = lax.axis_size("row")
    me = lax.axis_index("row")
    dbar = g[None]
    for u in reversed(range(len(conds))):
        m = masks[h + u]
        first = (me // m) % 2 == 0
        c = conds[u].reshape((-1,) + (1,) * (dbar.ndim - 1))
        kbar = jnp.where(c, dbar, 0.0)
        rbar = jnp.where(c, 0.0, dbar)
        sbar = lax.ppermute(rbar.astype(jnp.bfloat16), "row", xor_pairs(size, m)).astype(jnp.float32)
        pair = jnp.where(first, jnp.stack([kbar, sbar], 1), jnp.stack([sbar, kbar], 1))
        dbar = pair.reshape((-1,) + dbar.shape[1:])
    pick = (slots[:, None] == jnp.arange(1 << h, dtype=jnp.int32)[None, :]).astype(jnp.float32)
    hbar = jnp.sum(pick.reshape(pick.shape + (1,) * (dbar.ndim - 1)) * dbar[:, None], axis=0)
    for t in reversed(range(h)):
        m = masks[t]
        first = (me // m) % 2 == 0
        half = hbar.shape[0] // 2
        mine = jnp.where(first, hbar[:half], hbar[half:])
        other = jnp.where(first, hbar[half:], hbar[:half])
        hbar = mine + lax.ppermute(other.astype(jnp.bfloat16), "row", xor_pairs(size, m)).astype(jnp.float32)
    return hbar[0]


def embed(pre):
    return pre * lax.rsqrt(jnp.sum(pre * pre, axis=-1, keepdims=True) + 1e-06)


def body(
    node_feats,
    source_feats,
    nbr_blocks,
    nbr_count,
    adj_tiles,
    pos_index,
    noise_block_rows,
    w_self,
    w_neigh,
):
    rows = node_feats.shape[0]
    width = node_feats.shape[1]
    slots = adj_tiles.shape[1]
    highest = lax.Precision.HIGHEST
    nodes = rows * lax.axis_size("row") * lax.axis_size("col")
    scale_factor = 1.0 / softness_divisor
    valid = jnp.arange(slots, dtype=jnp.int32)[None, :] < nbr_count[:, None]
    tiles = adj_tiles * valid[:, :, None, None].astype(jnp.bfloat16)
    plan = route_plan(noise_block_rows)
    noise_feats = route_forward(node_feats[:NOISE], plan)
    piece = lax.all_gather(source_feats, "col", axis=0, tiled=True)
    piece, noise_feats = lax.optimization_barrier((piece, noise_feats))
    count = piece.shape[0] // BLOCK
    blocks = piece.reshape(count, BLOCK, width)

    def aggregate(part_tiles, part_ids):
        selected = jnp.take(blocks, part_ids, axis=0, mode="clip")
        summed = jnp.einsum("bkij,bkjd->bid", part_tiles, selected, preferred_element_type=jnp.float32)
        return summed.reshape(-1, width).astype(jnp.bfloat16)

    head = NOISE // BLOCK
    agg_head = aggregate(tiles[:head], nbr_blocks[:head])
    noise_agg = route_forward(agg_head, plan)
    agg = jnp.concatenate([agg_head, aggregate(tiles[head:], nbr_blocks[head:])], axis=0)
    all_feats = jnp.concatenate([node_feats, noise_feats], axis=0)
    all_agg = jnp.concatenate([agg, noise_agg], axis=0)
    pre = jnp.dot(all_feats, w_self, preferred_element_type=jnp.float32) + jnp.dot(
        all_agg, w_neigh, preferred_element_type=jnp.float32
    )
    emb32, pull = jax.vjp(embed, pre)
    all_bf = emb32.astype(jnp.bfloat16)
    zeta_bf = all_bf[:rows]
    noise_emb = all_bf[rows:].astype(jnp.float32)
    zeta = zeta_bf.astype(jnp.float32)
    pairing = (pos_index[:, None] == jnp.arange(rows, dtype=jnp.int32)[None, :]).astype(jnp.float32)
    partner = jnp.dot(pairing.astype(jnp.bfloat16), zeta_bf, preferred_element_type=jnp.float32)
    s_pos = jnp.sum(zeta * partner, axis=-1) * scale_factor
    s_neg = jnp.dot(zeta_bf, all_bf[rows:].T, preferred_element_type=jnp.float32) * scale_factor
    loss_part = (jnp.sum(jax.nn.softplus(-s_pos)) + jnp.sum(jax.nn.softplus(s_neg)) / NOISE) / nodes
    grad_pos = -jax.nn.sigmoid(-s_pos) / nodes
    grad_neg = jax.nn.sigmoid(s_neg) / (NOISE * nodes)
    anchor = scale_factor * (
        grad_pos[:, None] * partner + jnp.dot(grad_neg, noise_emb, precision=highest)
    )
    partner_grad = jnp.dot(pairing.T, scale_factor * grad_pos[:, None] * zeta, precision=highest)
    dnoise = scale_factor * jnp.dot(grad_neg.T, zeta, precision=highest)
    dnoise = dnoise.astype(jnp.bfloat16).astype(jnp.float32)
    dzeta = jnp.concatenate([anchor + partner_grad, dnoise], axis=0)
    gpre = pull(dzeta)[0].astype(jnp.bfloat16)
    part_self = jnp.dot(all_feats.T, gpre, preferred_element_type=jnp.float32)
    neighbour_partial = jnp.dot(all_agg.T, gpre, preferred_element_type=jnp.float32)
    stacked = jnp.concatenate([part_self, neighbour_partial], axis=0)
    total, loss_tile = tree_allreduce(stacked, jnp.broadcast_to(loss_part, (8, width)))
    grad_self = total[:width]
    neighbour_weight_gradient = total[width:]
    return (grad_self, neighbour_weight_gradient, loss_tile[0, 0])


def solution(mesh):
    in_specs = (
        P(("row", "col"), None),
        P("col", None),
        P(("row", "col"), None),
        P(("row", "col")),
        P(("row", "col"), None, None, None),
        P(("row", "col")),
        P(),
        P(),
        P(),
    )
    out_specs = (P(), P(), P())
    return jax.shard_map(body, mesh=mesh, in_specs=in_specs, out_specs=out_specs, check_vma=False)
```

```python
import jax
import jax.numpy as jnp
from jax import lax
from jax.sharding import PartitionSpec as P

BLOCK = 128
NOISE = 128


softness_divisor = 0.2


def xor_pairs(size, mask):
    return [(i, i ^ mask) for i in range(size)]


DOUBLING = ((16, 8, 4, 2, 1), (4, 2, 16, 8, 1))
BUTTERFLY = (("row", 1), ("row", 2), ("row", 4), ("row", 8))


def tree_allreduce(buf, extra):
    ways = lax.axis_size("col")
    me = lax.axis_index("col")
    orders = [[mask for mask in order if mask < ways] for order in DOUBLING]
    position = [sum(((j // mask) % 2) << t for t, mask in enumerate(orders[j % 2])) for j in range(ways)]
    rows = buf.shape[0] // ways
    chunks = buf.reshape(ways, rows, buf.shape[1])
    scattered = lax.all_to_all(chunks, "col", 0, 0, tiled=False).sum(axis=0)
    joined = jnp.concatenate([scattered, extra], axis=0)
    for axis, mask in BUTTERFLY:
        size = lax.axis_size(axis)
        if mask >= size:
            continue
        joined = joined + lax.ppermute(joined, axis, xor_pairs(size, mask))
    buf, extra = joined[:rows], joined[rows:]
    odd = me % 2 == 1
    for even_mask, odd_mask in zip(*orders):
        mask = jnp.where(odd, odd_mask, even_mask)
        bit = (me // mask) % 2
        held = buf.shape[0]
        pairs = [(i, i ^ (odd_mask if i % 2 else even_mask)) for i in range(ways)]
        got = lax.ppermute(jnp.concatenate([buf, extra], axis=0), "col", pairs)
        extra = extra + got[held:]
        out = jnp.zeros((2 * held,) + buf.shape[1:], buf.dtype)
        out = lax.dynamic_update_slice_in_dim(out, buf, bit * held, 0)
        out = lax.dynamic_update_slice_in_dim(out, got[:held], (1 - bit) * held, 0)
        buf = out
    buf = buf.reshape(ways, rows, buf.shape[1])[jnp.array(position, jnp.int32)].reshape(-1, buf.shape[1])
    return buf, extra


def route_plan(table):
    size = lax.axis_size("row")
    n = size.bit_length() - 1
    masks = [1 << (n - 1)] + [1 << i for i in range(n - 1)]
    h = n // 2
    me = lax.axis_index("row")
    high = sum(masks[:h])
    wide = 1 << (n - h)
    j = jnp.arange(wide, dtype=jnp.int32)
    dest = (me & high) + sum(((j >> i) & 1) * masks[h + i] for i in range(n - h))
    src = table[dest]
    slots = sum(((src // masks[i]) % 2) << i for i in range(h))
    conds = []
    for u in range(n - h):
        m = masks[h + u]
        k = jnp.arange(wide >> (u + 1), dtype=jnp.int32)
        done_bits = high + sum(masks[h:h + u + 1])
        kept = (me & done_bits) + sum(((k >> i) & 1) * masks[h + u + 1 + i] for i in range(n - h - u - 1))
        conds.append((table[kept] // m) % 2 == (me // m) % 2)
    return masks, h, slots, conds


def route_forward(x, plan):
    masks, h, slots, conds = plan
    size = lax.axis_size("row")
    me = lax.axis_index("row")
    held = x[None]
    for t in range(h):
        m = masks[t]
        got = lax.ppermute(held, "row", xor_pairs(size, m))
        first = (me // m) % 2 == 0
        held = jnp.where(first, jnp.concatenate([held, got], 0), jnp.concatenate([got, held], 0))
    d = jnp.take(held, slots, axis=0)
    for u, c in enumerate(conds):
        m = masks[h + u]
        first = (me // m) % 2 == 0
        pair = d.reshape((-1, 2) + d.shape[1:])
        keep = jnp.where(first, pair[:, 0], pair[:, 1])
        send = jnp.where(first, pair[:, 1], pair[:, 0])
        got = lax.ppermute(send, "row", xor_pairs(size, m))
        d = jnp.where(c.reshape((-1,) + (1,) * (d.ndim - 1)), keep, got)
    return d[0]


def route_backward(g, plan):
    masks, h, slots, conds = plan
    size = lax.axis_size("row")
    me = lax.axis_index("row")
    dbar = g[None]
    for u in reversed(range(len(conds))):
        m = masks[h + u]
        first = (me // m) % 2 == 0
        c = conds[u].reshape((-1,) + (1,) * (dbar.ndim - 1))
        kbar = jnp.where(c, dbar, 0.0)
        rbar = jnp.where(c, 0.0, dbar)
        sbar = lax.ppermute(rbar.astype(jnp.bfloat16), "row", xor_pairs(size, m)).astype(jnp.float32)
        pair = jnp.where(first, jnp.stack([kbar, sbar], 1), jnp.stack([sbar, kbar], 1))
        dbar = pair.reshape((-1,) + dbar.shape[1:])
    pick = (slots[:, None] == jnp.arange(1 << h, dtype=jnp.int32)[None, :]).astype(jnp.float32)
    hbar = jnp.sum(pick.reshape(pick.shape + (1,) * (dbar.ndim - 1)) * dbar[:, None], axis=0)
    for t in reversed(range(h)):
        m = masks[t]
        first = (me // m) % 2 == 0
        half = hbar.shape[0] // 2
        mine = jnp.where(first, hbar[:half], hbar[half:])
        other = jnp.where(first, hbar[half:], hbar[:half])
        hbar = mine + lax.ppermute(other.astype(jnp.bfloat16), "row", xor_pairs(size, m)).astype(jnp.float32)
    return hbar[0]


def embed(pre):
    return pre * lax.rsqrt(jnp.sum(pre * pre, axis=-1, keepdims=True) + 1e-06)


def body(
    node_feats,
    source_feats,
    nbr_blocks,
    nbr_count,
    adj_tiles,
    pos_index,
    noise_block_rows,
    w_self,
    w_neigh,
):
    rows = node_feats.shape[0]
    width = node_feats.shape[1]
    slots = adj_tiles.shape[1]
    highest = lax.Precision.HIGHEST
    nodes = rows * lax.axis_size("row") * lax.axis_size("col")
    scale_factor = 1.0 / softness_divisor
    valid = jnp.arange(slots, dtype=jnp.int32)[None, :] < nbr_count[:, None]
    tiles = adj_tiles * valid[:, :, None, None].astype(jnp.bfloat16)
    plan = route_plan(noise_block_rows)
    noise_feats = route_forward(node_feats[:NOISE], plan)
    piece = lax.all_gather(source_feats, "col", axis=0, tiled=True)
    piece, noise_feats = lax.optimization_barrier((piece, noise_feats))
    count = piece.shape[0] // BLOCK
    blocks = piece.reshape(count, BLOCK, width)

    def aggregate(part_tiles, part_ids):
        selected = jnp.take(blocks, part_ids, axis=0, mode="clip")
        summed = jnp.einsum("bkij,bkjd->bid", part_tiles, selected, preferred_element_type=jnp.float32)
        return summed.reshape(-1, width).astype(jnp.bfloat16)

    head = NOISE // BLOCK
    agg_head = aggregate(tiles[:head], nbr_blocks[:head])
    noise_agg = route_forward(agg_head, plan)
    agg = jnp.concatenate([agg_head, aggregate(tiles[head:], nbr_blocks[head:])], axis=0)
    all_feats = jnp.concatenate([node_feats, noise_feats], axis=0)
    all_agg = jnp.concatenate([agg, noise_agg], axis=0)
    pre = jnp.dot(all_feats, w_self, preferred_element_type=jnp.float32) + jnp.dot(
        all_agg, w_neigh, preferred_element_type=jnp.float32
    )
    emb32, pull = jax.vjp(embed, pre)
    all_bf = emb32.astype(jnp.bfloat16)
    zeta_bf = all_bf[:rows]
    noise_emb = all_bf[rows:].astype(jnp.float32)
    zeta = zeta_bf.astype(jnp.float32)
    pairing = (pos_index[:, None] == jnp.arange(rows, dtype=jnp.int32)[None, :]).astype(jnp.float32)
    partner = jnp.dot(pairing.astype(jnp.bfloat16), zeta_bf, preferred_element_type=jnp.float32)
    s_pos = jnp.sum(zeta * partner, axis=-1) * scale_factor
    s_neg = jnp.dot(zeta_bf, all_bf[rows:].T, preferred_element_type=jnp.float32) * scale_factor
    loss_part = (jnp.sum(jax.nn.softplus(-s_pos)) + jnp.sum(jax.nn.softplus(s_neg)) / NOISE) / nodes
    grad_pos = -jax.nn.sigmoid(-s_pos) / nodes
    grad_neg = jax.nn.sigmoid(s_neg) / (NOISE * nodes)
    anchor = scale_factor * (
        grad_pos[:, None] * partner + jnp.dot(grad_neg, noise_emb, precision=highest)
    )
    partner_grad = jnp.dot(pairing.T, scale_factor * grad_pos[:, None] * zeta, precision=highest)
    dnoise = scale_factor * jnp.dot(grad_neg.T, zeta, precision=highest)
    dnoise = dnoise.astype(jnp.bfloat16).astype(jnp.float32)
    dzeta = jnp.concatenate([anchor + partner_grad, dnoise], axis=0)
    gpre = pull(dzeta)[0].astype(jnp.bfloat16)
    part_self = jnp.dot(all_feats.T, gpre, preferred_element_type=jnp.float32)
    neighbour_partial = jnp.dot(all_agg.T, gpre, preferred_element_type=jnp.float32)
    stacked = jnp.concatenate([part_self, neighbour_partial], axis=0)
    total, loss_tile = tree_allreduce(stacked, jnp.broadcast_to(loss_part, (8, width)))
    grad_self = total[:width]
    neighbour_weight_gradient = total[width:]
    return (grad_self, neighbour_weight_gradient, loss_tile[0, 0])


def solution(mesh):
    in_specs = (
        P(("row", "col"), None),
        P("col", None),
        P(("row", "col"), None),
        P(("row", "col")),
        P(("row", "col"), None, None, None),
        P(("row", "col")),
        P(),
        P(),
        P(),
    )
    out_specs = (P(), P(), P())
    return jax.shard_map(body, mesh=mesh, in_specs=in_specs, out_specs=out_specs, check_vma=False)
```

```python
import jax
import jax.numpy as jnp
from jax import lax
from jax.sharding import PartitionSpec as P

BLOCK = 128
NOISE = 128


softness_divisor = 0.2


def xor_pairs(size, mask):
    return [(i, i ^ mask) for i in range(size)]


DOUBLING = ((16, 8, 4, 2, 1), (4, 2, 16, 8, 1))
BUTTERFLY = (("row", 1), ("row", 2), ("row", 4), ("row", 8))


def tree_allreduce(buf, extra):
    ways = lax.axis_size("col")
    me = lax.axis_index("col")
    orders = [[mask for mask in order if mask < ways] for order in DOUBLING]
    position = [sum(((j // mask) % 2) << t for t, mask in enumerate(orders[j % 2])) for j in range(ways)]
    rows = buf.shape[0] // ways
    chunks = buf.reshape(ways, rows, buf.shape[1])[jnp.array(position, jnp.int32)]
    scattered = lax.all_to_all(chunks, "col", 0, 0, tiled=False).sum(axis=0)
    joined = jnp.concatenate([scattered, extra], axis=0)
    for axis, mask in BUTTERFLY:
        size = lax.axis_size(axis)
        if mask >= size:
            continue
        joined = joined + lax.ppermute(joined, axis, xor_pairs(size, mask))
    buf, extra = joined[:rows], joined[rows:]
    odd = me % 2 == 1
    for even_mask, odd_mask in zip(*orders):
        mask = jnp.where(odd, odd_mask, even_mask)
        bit = (me // mask) % 2
        held = buf.shape[0]
        pairs = [(i, i ^ (odd_mask if i % 2 else even_mask)) for i in range(ways)]
        got = lax.ppermute(jnp.concatenate([buf, extra], axis=0), "col", pairs)
        extra = extra + got[held:]
        out = jnp.zeros((2 * held,) + buf.shape[1:], buf.dtype)
        out = lax.dynamic_update_slice_in_dim(out, buf, bit * held, 0)
        out = lax.dynamic_update_slice_in_dim(out, got[:held], (1 - bit) * held, 0)
        buf = out
    return buf, extra


def route_plan(table):
    size = lax.axis_size("row")
    n = size.bit_length() - 1
    masks = [1 << (n - 1)] + [1 << i for i in range(n - 1)]
    h = n // 2
    me = lax.axis_index("row")
    high = sum(masks[:h])
    wide = 1 << (n - h)
    j = jnp.arange(wide, dtype=jnp.int32)
    dest = (me & high) + sum(((j >> i) & 1) * masks[h + i] for i in range(n - h))
    src = table[dest]
    slots = sum(((src // masks[i]) % 2) << i for i in range(h))
    conds = []
    for u in range(n - h):
        m = masks[h + u]
        k = jnp.arange(wide >> (u + 1), dtype=jnp.int32)
        done_bits = high + sum(masks[h:h + u + 1])
        kept = (me & done_bits) + sum(((k >> i) & 1) * masks[h + u + 1 + i] for i in range(n - h - u - 1))
        conds.append((table[kept] // m) % 2 == (me // m) % 2)
    return masks, h, slots, conds


def route_forward(x, plan):
    masks, h, slots, conds = plan
    size = lax.axis_size("row")
    me = lax.axis_index("row")
    held = x[None]
    for t in range(h):
        m = masks[t]
        got = lax.ppermute(held, "row", xor_pairs(size, m))
        first = (me // m) % 2 == 0
        held = jnp.where(first, jnp.concatenate([held, got], 0), jnp.concatenate([got, held], 0))
    d = jnp.take(held, slots, axis=0)
    for u, c in enumerate(conds):
        m = masks[h + u]
        first = (me // m) % 2 == 0
        pair = d.reshape((-1, 2) + d.shape[1:])
        keep = jnp.where(first, pair[:, 0], pair[:, 1])
        send = jnp.where(first, pair[:, 1], pair[:, 0])
        got = lax.ppermute(send, "row", xor_pairs(size, m))
        d = jnp.where(c.reshape((-1,) + (1,) * (d.ndim - 1)), keep, got)
    return d[0]


def route_backward(g, plan):
    masks, h, slots, conds = plan
    size = lax.axis_size("row")
    me = lax.axis_index("row")
    dbar = g[None]
    for u in reversed(range(len(conds))):
        m = masks[h + u]
        first = (me // m) % 2 == 0
        c = conds[u].reshape((-1,) + (1,) * (dbar.ndim - 1))
        kbar = jnp.where(c, dbar, 0.0)
        rbar = jnp.where(c, 0.0, dbar)
        sbar = lax.ppermute(rbar.astype(jnp.bfloat16), "row", xor_pairs(size, m)).astype(jnp.float32)
        pair = jnp.where(first, jnp.stack([kbar, sbar], 1), jnp.stack([sbar, kbar], 1))
        dbar = pair.reshape((-1,) + dbar.shape[1:])
    pick = (slots[:, None] == jnp.arange(1 << h, dtype=jnp.int32)[None, :]).astype(jnp.float32)
    hbar = jnp.sum(pick.reshape(pick.shape + (1,) * (dbar.ndim - 1)) * dbar[:, None], axis=0)
    for t in reversed(range(h)):
        m = masks[t]
        first = (me // m) % 2 == 0
        half = hbar.shape[0] // 2
        mine = jnp.where(first, hbar[:half], hbar[half:])
        other = jnp.where(first, hbar[half:], hbar[:half])
        hbar = mine + lax.ppermute(other.astype(jnp.bfloat16), "row", xor_pairs(size, m)).astype(jnp.float32)
    return hbar[0]


def exact_dot(wide, narrow):
    high = wide.astype(jnp.bfloat16)
    low = (wide - high.astype(jnp.float32)).astype(jnp.bfloat16)
    return jnp.dot(high, narrow, preferred_element_type=jnp.float32) + jnp.dot(
        low, narrow, preferred_element_type=jnp.float32
    )


def embed(pre):
    return pre * lax.rsqrt(jnp.sum(pre * pre, axis=-1, keepdims=True) + 1e-06)


def body(
    node_feats,
    source_feats,
    nbr_blocks,
    nbr_count,
    adj_tiles,
    pos_index,
    noise_block_rows,
    w_self,
    w_neigh,
):
    rows = node_feats.shape[0]
    width = node_feats.shape[1]
    slots = adj_tiles.shape[1]
    highest = lax.Precision.HIGHEST
    nodes = rows * lax.axis_size("row") * lax.axis_size("col")
    scale_factor = 1.0 / softness_divisor
    valid = jnp.arange(slots, dtype=jnp.int32)[None, :] < nbr_count[:, None]
    tiles = adj_tiles * valid[:, :, None, None].astype(jnp.bfloat16)
    plan = route_plan(noise_block_rows)
    noise_feats = route_forward(node_feats[:NOISE], plan)
    piece = lax.all_gather(source_feats, "col", axis=0, tiled=True)
    piece, noise_feats = lax.optimization_barrier((piece, noise_feats))
    count = piece.shape[0] // BLOCK
    blocks = piece.reshape(count, BLOCK, width)

    def aggregate(part_tiles, part_ids):
        selected = jnp.take(blocks, part_ids, axis=0, mode="clip")
        summed = jnp.einsum("bkij,bkjd->bid", part_tiles, selected, preferred_element_type=jnp.float32)
        return summed.reshape(-1, width).astype(jnp.bfloat16)

    head = NOISE // BLOCK
    agg_head = aggregate(tiles[:head], nbr_blocks[:head])
    noise_agg = route_forward(agg_head, plan)
    agg = jnp.concatenate([agg_head, aggregate(tiles[head:], nbr_blocks[head:])], axis=0)
    all_feats = jnp.concatenate([node_feats, noise_feats], axis=0)
    all_agg = jnp.concatenate([agg, noise_agg], axis=0)
    pre = jnp.dot(all_feats, w_self, preferred_element_type=jnp.float32) + jnp.dot(
        all_agg, w_neigh, preferred_element_type=jnp.float32
    )
    emb32, pull = jax.vjp(embed, pre)
    all_bf = emb32.astype(jnp.bfloat16)
    zeta_bf = all_bf[:rows]
    noise_emb = all_bf[rows:].astype(jnp.float32)
    zeta = zeta_bf.astype(jnp.float32)
    pairing = (pos_index[:, None] == jnp.arange(rows, dtype=jnp.int32)[None, :]).astype(jnp.float32)
    partner = jnp.dot(pairing.astype(jnp.bfloat16), zeta_bf, preferred_element_type=jnp.float32)
    s_pos = jnp.sum(zeta * partner, axis=-1) * scale_factor
    s_neg = jnp.dot(zeta_bf, all_bf[rows:].T, preferred_element_type=jnp.float32) * scale_factor
    loss_part = (jnp.sum(jax.nn.softplus(-s_pos)) + jnp.sum(jax.nn.softplus(s_neg)) / NOISE) / nodes
    grad_pos = -jax.nn.sigmoid(-s_pos) / nodes
    grad_neg = jax.nn.sigmoid(s_neg) / (NOISE * nodes)
    anchor = scale_factor * (
        grad_pos[:, None] * partner + exact_dot(grad_neg, noise_emb.astype(jnp.bfloat16))
    )
    partner_grad = exact_dot((scale_factor * grad_pos[:, None] * zeta).T, pairing.astype(jnp.bfloat16)).T
    dnoise = scale_factor * exact_dot(grad_neg.T, zeta_bf)
    dnoise = dnoise.astype(jnp.bfloat16).astype(jnp.float32)
    dzeta = jnp.concatenate([anchor + partner_grad, dnoise], axis=0)
    gpre = pull(dzeta)[0].astype(jnp.bfloat16)
    part_self = jnp.dot(all_feats.T, gpre, preferred_element_type=jnp.float32)
    neighbour_partial = jnp.dot(all_agg.T, gpre, preferred_element_type=jnp.float32)
    stacked = jnp.concatenate([part_self, neighbour_partial], axis=0)
    total, loss_tile = tree_allreduce(stacked, jnp.broadcast_to(loss_part, (8, width)))
    grad_self = total[:width]
    neighbour_weight_gradient = total[width:]
    return (grad_self, neighbour_weight_gradient, loss_tile[0, 0])


def solution(mesh):
    in_specs = (
        P(("row", "col"), None),
        P("col", None),
        P(("row", "col"), None),
        P(("row", "col")),
        P(("row", "col"), None, None, None),
        P(("row", "col")),
        P(),
        P(),
        P(),
    )
    out_specs = (P(), P(), P())
    return jax.shard_map(body, mesh=mesh, in_specs=in_specs, out_specs=out_specs, check_vma=False)
```

```python
import jax
import jax.numpy as jnp
from jax import lax
from jax.sharding import PartitionSpec as P

BLOCK = 128
NOISE = 128


softness_divisor = 0.2


def xor_pairs(size, mask):
    return [(i, i ^ mask) for i in range(size)]


DOUBLING = ((16, 8, 4, 2, 1), (4, 2, 16, 8, 1))
BUTTERFLY = (("row", 1), ("row", 2), ("row", 4), ("row", 8))


def tree_allreduce(buf, extra):
    ways = lax.axis_size("col")
    me = lax.axis_index("col")
    orders = [[mask for mask in order if mask < ways] for order in DOUBLING]
    position = [sum(((j // mask) % 2) << t for t, mask in enumerate(orders[j % 2])) for j in range(ways)]
    rows = buf.shape[0] // ways
    chunks = buf.reshape(ways, rows, buf.shape[1])[jnp.array(position, jnp.int32)]
    scattered = lax.all_to_all(chunks, "col", 0, 0, tiled=False).sum(axis=0)
    joined = jnp.concatenate([scattered, extra], axis=0)
    for axis, mask in BUTTERFLY:
        size = lax.axis_size(axis)
        if mask >= size:
            continue
        joined = joined + lax.ppermute(joined, axis, xor_pairs(size, mask))
    buf, extra = joined[:rows], joined[rows:]
    odd = me % 2 == 1
    steps = list(zip(*orders))
    for even_mask, odd_mask in steps:
        mask = jnp.where(odd, odd_mask, even_mask)
        bit = (me // mask) % 2
        held = buf.shape[0]
        pairs = [(i, i ^ (odd_mask if i % 2 else even_mask)) for i in range(ways)]
        got = lax.ppermute(jnp.concatenate([buf, extra], axis=0), "col", pairs)
        extra = extra + got[held:]
        if (even_mask, odd_mask) == steps[-1]:
            mine_first = bit == 0
            return jnp.where(mine_first, buf, got[:held]), jnp.where(mine_first, got[:held], buf), extra
        out = jnp.zeros((2 * held,) + buf.shape[1:], buf.dtype)
        out = lax.dynamic_update_slice_in_dim(out, buf, bit * held, 0)
        out = lax.dynamic_update_slice_in_dim(out, got[:held], (1 - bit) * held, 0)
        buf = out


def route_plan(table):
    size = lax.axis_size("row")
    n = size.bit_length() - 1
    masks = [1 << (n - 1)] + [1 << i for i in range(n - 1)]
    h = n // 2
    me = lax.axis_index("row")
    high = sum(masks[:h])
    wide = 1 << (n - h)
    j = jnp.arange(wide, dtype=jnp.int32)
    dest = (me & high) + sum(((j >> i) & 1) * masks[h + i] for i in range(n - h))
    src = table[dest]
    slots = sum(((src // masks[i]) % 2) << i for i in range(h))
    conds = []
    for u in range(n - h):
        m = masks[h + u]
        k = jnp.arange(wide >> (u + 1), dtype=jnp.int32)
        done_bits = high + sum(masks[h:h + u + 1])
        kept = (me & done_bits) + sum(((k >> i) & 1) * masks[h + u + 1 + i] for i in range(n - h - u - 1))
        conds.append((table[kept] // m) % 2 == (me // m) % 2)
    return masks, h, slots, conds


def route_forward(x, plan):
    masks, h, slots, conds = plan
    size = lax.axis_size("row")
    me = lax.axis_index("row")
    held = x[None]
    for t in range(h):
        m = masks[t]
        got = lax.ppermute(held, "row", xor_pairs(size, m))
        first = (me // m) % 2 == 0
        held = jnp.where(first, jnp.concatenate([held, got], 0), jnp.concatenate([got, held], 0))
    d = jnp.take(held, slots, axis=0)
    for u, c in enumerate(conds):
        m = masks[h + u]
        first = (me // m) % 2 == 0
        pair = d.reshape((-1, 2) + d.shape[1:])
        keep = jnp.where(first, pair[:, 0], pair[:, 1])
        send = jnp.where(first, pair[:, 1], pair[:, 0])
        got = lax.ppermute(send, "row", xor_pairs(size, m))
        d = jnp.where(c.reshape((-1,) + (1,) * (d.ndim - 1)), keep, got)
    return d[0]


def route_backward(g, plan):
    masks, h, slots, conds = plan
    size = lax.axis_size("row")
    me = lax.axis_index("row")
    dbar = g[None]
    for u in reversed(range(len(conds))):
        m = masks[h + u]
        first = (me // m) % 2 == 0
        c = conds[u].reshape((-1,) + (1,) * (dbar.ndim - 1))
        kbar = jnp.where(c, dbar, 0.0)
        rbar = jnp.where(c, 0.0, dbar)
        sbar = lax.ppermute(rbar.astype(jnp.bfloat16), "row", xor_pairs(size, m)).astype(jnp.float32)
        pair = jnp.where(first, jnp.stack([kbar, sbar], 1), jnp.stack([sbar, kbar], 1))
        dbar = pair.reshape((-1,) + dbar.shape[1:])
    pick = (slots[:, None] == jnp.arange(1 << h, dtype=jnp.int32)[None, :]).astype(jnp.float32)
    hbar = jnp.sum(pick.reshape(pick.shape + (1,) * (dbar.ndim - 1)) * dbar[:, None], axis=0)
    for t in reversed(range(h)):
        m = masks[t]
        first = (me // m) % 2 == 0
        half = hbar.shape[0] // 2
        mine = jnp.where(first, hbar[:half], hbar[half:])
        other = jnp.where(first, hbar[half:], hbar[:half])
        hbar = mine + lax.ppermute(other.astype(jnp.bfloat16), "row", xor_pairs(size, m)).astype(jnp.float32)
    return hbar[0]


def embed(pre):
    return pre * lax.rsqrt(jnp.sum(pre * pre, axis=-1, keepdims=True) + 1e-06)


def body(
    node_feats,
    source_feats,
    nbr_blocks,
    nbr_count,
    adj_tiles,
    pos_index,
    noise_block_rows,
    w_self,
    w_neigh,
):
    rows = node_feats.shape[0]
    width = node_feats.shape[1]
    slots = adj_tiles.shape[1]
    highest = lax.Precision.HIGHEST
    nodes = rows * lax.axis_size("row") * lax.axis_size("col")
    scale_factor = 1.0 / softness_divisor
    valid = jnp.arange(slots, dtype=jnp.int32)[None, :] < nbr_count[:, None]
    tiles = adj_tiles * valid[:, :, None, None].astype(jnp.bfloat16)
    plan = route_plan(noise_block_rows)
    noise_feats = route_forward(node_feats[:NOISE], plan)
    piece = lax.all_gather(source_feats, "col", axis=0, tiled=True)
    piece, noise_feats = lax.optimization_barrier((piece, noise_feats))
    count = piece.shape[0] // BLOCK
    blocks = piece.reshape(count, BLOCK, width)

    def aggregate(part_tiles, part_ids):
        selected = jnp.take(blocks, part_ids, axis=0, mode="clip")
        summed = jnp.einsum("bkij,bkjd->bid", part_tiles, selected, preferred_element_type=jnp.float32)
        return summed.reshape(-1, width).astype(jnp.bfloat16)

    head = NOISE // BLOCK
    agg_head = aggregate(tiles[:head], nbr_blocks[:head])
    noise_agg = route_forward(agg_head, plan)
    agg = jnp.concatenate([agg_head, aggregate(tiles[head:], nbr_blocks[head:])], axis=0)
    all_feats = jnp.concatenate([node_feats, noise_feats], axis=0)
    all_agg = jnp.concatenate([agg, noise_agg], axis=0)
    pre = jnp.dot(all_feats, w_self, preferred_element_type=jnp.float32) + jnp.dot(
        all_agg, w_neigh, preferred_element_type=jnp.float32
    )
    emb32, pull = jax.vjp(embed, pre)
    all_bf = emb32.astype(jnp.bfloat16)
    zeta_bf = all_bf[:rows]
    noise_emb = all_bf[rows:].astype(jnp.float32)
    zeta = zeta_bf.astype(jnp.float32)
    pairing = (pos_index[:, None] == jnp.arange(rows, dtype=jnp.int32)[None, :]).astype(jnp.float32)
    partner = jnp.dot(pairing.astype(jnp.bfloat16), zeta_bf, preferred_element_type=jnp.float32)
    s_pos = jnp.sum(zeta * partner, axis=-1) * scale_factor
    s_neg = jnp.dot(zeta_bf, all_bf[rows:].T, preferred_element_type=jnp.float32) * scale_factor
    loss_part = (jnp.sum(jax.nn.softplus(-s_pos)) + jnp.sum(jax.nn.softplus(s_neg)) / NOISE) / nodes
    grad_pos = -jax.nn.sigmoid(-s_pos) / nodes
    grad_neg = jax.nn.sigmoid(s_neg) / (NOISE * nodes)
    anchor = scale_factor * (
        grad_pos[:, None] * partner + jnp.dot(grad_neg, noise_emb, precision=highest)
    )
    partner_grad = jnp.dot(pairing.T, scale_factor * grad_pos[:, None] * zeta, precision=highest)
    dnoise = scale_factor * jnp.dot(grad_neg.T, zeta, precision=highest)
    dnoise = dnoise.astype(jnp.bfloat16).astype(jnp.float32)
    dzeta = jnp.concatenate([anchor + partner_grad, dnoise], axis=0)
    gpre = pull(dzeta)[0].astype(jnp.bfloat16)
    part_self = jnp.dot(all_feats.T, gpre, preferred_element_type=jnp.float32)
    neighbour_partial = jnp.dot(all_agg.T, gpre, preferred_element_type=jnp.float32)
    stacked = jnp.concatenate([part_self, neighbour_partial], axis=0)
    grad_self, neighbour_weight_gradient, loss_tile = tree_allreduce(stacked, jnp.broadcast_to(loss_part, (8, width)))
    return (grad_self, neighbour_weight_gradient, loss_tile[0, 0])


def solution(mesh):
    in_specs = (
        P(("row", "col"), None),
        P("col", None),
        P(("row", "col"), None),
        P(("row", "col")),
        P(("row", "col"), None, None, None),
        P(("row", "col")),
        P(),
        P(),
        P(),
    )
    out_specs = (P(), P(), P())
    return jax.shard_map(body, mesh=mesh, in_specs=in_specs, out_specs=out_specs, check_vma=False)
```
